256 devices in a mesh: gx: 8 (over x, core), yz: 32 (over z, y).
Axes of the slice: x: 4, y: 4, z: 8, core: 2. Of those that a mesh axis runs over, the one named last changes fastest.
Arguments:
- velocity: float32 [3, 256, 512, 128], P(None, 'gx', 'yz'), may hold values from -6 to 6
- old_pressure: float32 [256, 512, 128], P('gx', 'yz'), may hold values from -3 to 3
- delta_weight: bfloat16 [8, 1024, 128, 128], P('gx', 'yz'), may hold values from -0.5 to 0.5
- marker_target: float32 [8, 1024, 3, 128], P('gx', 'yz'), may hold values from -6 to 6
- pair_owner: int32 [8, 1024, 1], P('gx', 'yz'), may hold values from 0 to 31; in each aligned block of 32 rows (0 to 31, 32 to 63, ..., all dimensions but the last counted through in order) at most 4 rows name the same one
- pair_grain: int32 [8, 1024], P('gx', 'yz'), may hold values from 0 to 31
- box_anchor: int32 [8, 1024, 3], P('gx', 'yz'), may hold values from 0 to 120, as said below
Outputs:
- new_velocity: float32 [3, 256, 512, 128], P(None, 'gx', 'yz')
- pressure: float32 [256, 512, 128], P('gx', 'yz')
The draws below stay inside these ranges and needn't reach their ends.
Inputs may be any that keep to these rules, and one draw needn't show every extreme that they name: Block r of slab i lies on tile r // 32 of that slab; its grain is owned by tile pair_owner of the same slab. Among the 32 blocks of one tile at most 4 name the same owner, and some tile reaches 4. `pair_grain`: blocks of one slab with equal owner and grain slot belong to one grain. `box_anchor`: column 0 is at most 28, column 1 at most 12, column 2 at most 120, and each of these is reached, so every box lies inside its tile.
All inputs are finite; a program needn't handle non-finite values.
Results may differ from the reference program's by a relative error of at most 0.002.
Values may be sent and summed in bfloat16 or wider, within the bound.
No kernel may reach another device: no remote copies, remote signals or barrier semaphores. Data moves between devices by JAX's collectives and lax.ppermute only.
A program may use at most 128 MiB of HBM per device.

```python
import math
import jax
import jax.numpy as jnp
import numpy as np
from jax import lax

CX = 32
CZ = 16
NY = 128
BX = 4
BZ = 4
BY = 8
BOX = 128
M = 128
P_SIZE = 32
GO = 32
S = 4
SWEEPS = 2
NX = 256
NZ = 512
N_GX = 8
N_YZ = 32


def draw_box_anchor(key, part):
    row_total = N_GX * N_YZ * P_SIZE
    streams = jax.random.split(key, 3)
    first = jax.random.randint(streams[0], (row_total,), 0, CX - BX + 1)
    second = jax.random.randint(streams[1], (row_total,), 0, CZ - BZ + 1)
    third = jax.random.randint(streams[2], (row_total,), 0, NY - BY + 1)
    corner = jnp.arange(row_total) % P_SIZE == 0
    first = jnp.where(corner, CX - BX, first)
    second = jnp.where(corner, CZ - BZ, second)
    third = jnp.where(corner, NY - BY, third)
    return jnp.stack([first, second, third], axis=-1).reshape(N_GX, N_YZ * P_SIZE, 3).astype(jnp.int32)


def plant(entries, own_key, low, largest):
    shape = entries.shape
    index_at = [jax.random.randint(jax.random.fold_in(own_key, axis), (), 0, shape[axis]) for axis in range(len(shape))]
    entries = entries.at[tuple(index_at)].set(low)
    longest = shape.index(max(shape))
    index_at[longest] = (index_at[longest] + 1) % shape[longest]
    return entries.at[tuple(index_at)].set(largest)


def levels(own_key, dims, cuts, low, high):
    def one(axis_at, shards_of):
        heights = jax.random.uniform(jax.random.fold_in(jax.random.fold_in(own_key, 6), axis_at), (shards_of,), jnp.float32, low / len(cuts), high / len(cuts))
        return jnp.repeat(jnp.exp(heights), dims[axis_at] // shards_of).reshape((-1,) + (1,) * (len(dims) - axis_at - 1))

    factor_of = one(*cuts[0])
    for cut in cuts[1:]:
        factor_of = factor_of * one(*cut)
    return factor_of


def deal_out(stream_key, own, number, rows, count, top, limit, skew):
    sequence = jax.random.permutation(stream_key, count)
    heavy_load, common = load_shares(count, rows * top, limit, skew, True), load_shares(count, rows * top, limit, skew, False)
    places = jnp.arange(count)

    def named(lengths, rotation):
        used = int((lengths > 0).sum())
        fixed = max(1, used // 4)
        passed = fixed + (places - fixed + rotation * (used - fixed)) % max(1, count - fixed)
        return jnp.zeros((count,), jnp.int32).at[sequence[jnp.where(places < fixed, places, passed)]].set(jnp.asarray(lengths, jnp.int32))

    lengths = jnp.where(number % 4 == 0, named(heavy_load, number // 4), named(common, number - number // 4 - 1))
    mixed = jax.random.permutation(jax.random.fold_in(own, 3), count)
    donor, taker = mixed[0:count // 2 * 2:2], mixed[1:count // 2 * 2:2]
    margin = jnp.minimum(lengths[donor] - 1, limit - lengths[taker]) // 2
    margin = jnp.where((donor == sequence[0]) | (taker == sequence[0]) | (lengths[taker] == 0), 0, jnp.maximum(margin, 0))
    passed = jax.random.randint(jax.random.fold_in(own, 4), (count // 2,), 0, 1 << 20) % (margin + 1)
    lengths = lengths.at[donor].add(-passed).at[taker].add(passed)
    members = jnp.searchsorted(jnp.cumsum(lengths), jnp.arange(rows * top), side="right").astype(jnp.int32)
    listing = members.reshape(top, rows).T
    listing = listing[jax.random.permutation(jax.random.fold_in(own, 1), rows)]
    rotation = jax.random.randint(jax.random.fold_in(own, 2), (rows, 1), 0, top)
    return jnp.take_along_axis(listing, (jnp.arange(top)[None, :] + rotation) % top, axis=1)


def load_shares(count, total, reach, slope, full):
    loads = [(1 << 20) // math.isqrt(grade ** slope) + 1 for grade in range(1, count + 1)]
    largest = reach if full else min(reach, max(-(-total // count), total * loads[0] // sum(loads)))
    least = 1 if total - largest >= count - 1 else 0
    holding, rest = [largest] + [least] * (count - 1), total - largest - least * (count - 1)
    while rest > 0:
        candidates = [i for i in range(1, count) if holding[i] < largest] or [i for i in range(1, count) if holding[i] < reach]
        whole, left = sum([loads[i] for i in candidates]), rest
        for i in candidates:
            addition = min(reach - holding[i], max(1, left * loads[i] // whole), rest)
            holding[i] = holding[i] + addition
            rest = rest - addition
    return np.array(holding)


def gaussian(stream_key, shape, width, reach, cuts=(), kind=jnp.bfloat16):
    level = levels(stream_key, shape, cuts, -0.22, 0.18) if cuts else 1.0
    entries = jax.random.normal(stream_key, shape, jnp.float32) * width * level
    return jnp.minimum(jnp.maximum(entries, -reach), reach).astype(kind)


def setup_inputs(seed: int = 0) -> dict:
    seeds = jax.random.split(jax.random.key(seed), 8)
    velocity = gaussian(seeds[0], (3, NX, NZ, NY), 1.0, 6.0, ((1, 8), (2, 32)), jnp.float32)
    old_pressure = gaussian(seeds[1], (NX, NZ, NY), 0.5, 3.0, ((0, 8), (1, 32)), jnp.float32)
    delta_weight = gaussian(seeds[2], (N_GX, N_YZ * P_SIZE, M, BOX), BOX ** -0.5, 0.5, ((0, 8), (1, 32)))
    marker_target = gaussian(seeds[3], (N_GX, N_YZ * GO, 3, M), 1.0, 6.0, ((0, 8), (1, 32)), jnp.float32)
    pair_owner_keys = jax.random.split(jax.random.fold_in(seeds[4], 1), N_GX * (N_YZ * P_SIZE) // P_SIZE)
    pair_owner_turns = jax.random.permutation(jax.random.fold_in(seeds[4], 3), N_GX * (N_YZ * P_SIZE) // P_SIZE)
    pair_owner = jax.vmap(lambda own, number: deal_out(jax.random.fold_in(seeds[4], 2), own, number, P_SIZE, N_YZ, 1, S, 2))(pair_owner_keys, pair_owner_turns).reshape((N_GX, N_YZ * P_SIZE, 1))
    pair_grain = plant(jax.random.randint(seeds[5], (N_GX, N_YZ * P_SIZE), 0, GO), jax.random.fold_in(seeds[5], 1), 0, GO - 1).astype(jnp.int32)
    box_anchor = draw_box_anchor(jax.random.fold_in(seeds[7], 71), 0)
    return dict(velocity=velocity, old_pressure=old_pressure, delta_weight=delta_weight, marker_target=marker_target, pair_owner=pair_owner, pair_grain=pair_grain, box_anchor=box_anchor)


step_size = 0.1
viscosity = 1.5


def extend(field):
    wrapped = jnp.concatenate([field[..., -1:, :, :], field, field[..., :1, :, :]], axis=-3)
    widths = [(0, 0)] * (field.ndim - 2) + [(1, 1), (0, 0)]
    return jnp.pad(wrapped, widths)


def inner(padded):
    return padded[..., 1:-1, 1:-1, :]


def along_x(padded):
    return 0.5 * (padded[..., 2:, 1:-1, :] - padded[..., :-2, 1:-1, :])


def along_z(padded):
    return 0.5 * (padded[..., 1:-1, 2:, :] - padded[..., 1:-1, :-2, :])


def along_y(field):
    return 0.5 * (jnp.roll(field, -1, -1) - jnp.roll(field, 1, -1))


def neighbours(padded):
    middle = inner(padded)
    total = padded[..., 2:, 1:-1, :] + padded[..., :-2, 1:-1, :]
    total = total + padded[..., 1:-1, 2:, :] + padded[..., 1:-1, :-2, :]
    return total + jnp.roll(middle, 1, -1) + jnp.roll(middle, -1, -1)


def gradient_of(padded):
    middle = inner(padded)
    return jnp.stack([along_x(padded), along_y(middle), along_z(padded)])


def predict(flow_padded):
    velocity_padded = flow_padded[:3]
    pressure_padded = flow_padded[3]
    current = inner(velocity_padded)
    laplace = neighbours(velocity_padded) - 6.0 * current
    advect = current[0] * along_x(velocity_padded)
    return current + step_size * (viscosity * laplace - advect) - gradient_of(pressure_padded)


def kernel_box_cells(anchors, box_x, box_z, box_y):
    steps_x = jnp.arange(box_x, dtype=jnp.int32)
    steps_z = jnp.arange(box_z, dtype=jnp.int32)
    steps_y = jnp.arange(box_y, dtype=jnp.int32)
    cell_x = anchors[:, 0, None, None, None] + steps_x[None, :, None, None]
    cell_z = anchors[:, 1, None, None, None] + steps_z[None, None, :, None]
    cell_y = anchors[:, 2, None, None, None] + steps_y[None, None, None, :]
    return cell_x, cell_z, cell_y


def reference(velocity, old_pressure, delta_weight, marker_target, pair_owner, pair_grain, box_anchor):
    flow_fields = jnp.concatenate([velocity, old_pressure[None]], 0)
    predicted = predict(extend(flow_fields))
    slab_number = jnp.arange(N_GX, dtype=jnp.int32)[:, None]
    row_number = jnp.arange(N_YZ * P_SIZE, dtype=jnp.int32)[None, :]
    offset_streamwise = jnp.broadcast_to(slab_number * CX, (N_GX, N_YZ * P_SIZE))
    shift_z = jnp.broadcast_to((row_number // P_SIZE) * CZ, (N_GX, N_YZ * P_SIZE))
    shift_y = jnp.zeros((N_GX, N_YZ * P_SIZE), jnp.int32)
    anchors = (box_anchor + jnp.stack([offset_streamwise, shift_z, shift_y], -1)).reshape(-1, 3).astype(jnp.int32)
    cell_x, cell_z, cell_y = kernel_box_cells(anchors, BX, BZ, BY)
    pair_total = anchors.shape[0]
    kernel_box_values = predicted[:, cell_x, cell_z, cell_y].astype(jnp.bfloat16).reshape(3, pair_total, BOX)
    delta_weights = delta_weight.reshape(pair_total, M, BOX).astype(jnp.float32)
    partial_force_value = jnp.einsum("eky,iey->eik", delta_weights, lax.optimization_barrier(kernel_box_values).astype(jnp.float32), precision=lax.Precision.HIGHEST)
    grain_keys = (slab_number * (N_YZ * GO) + pair_owner[..., 0] * GO + pair_grain).reshape(-1).astype(jnp.int32)
    marker_velocity = jax.ops.segment_sum(partial_force_value, grain_keys, num_segments=N_GX * N_YZ * GO)
    grain_force = (marker_target.reshape(-1, 3, M) - marker_velocity).astype(jnp.bfloat16)
    marker_pair_force = lax.optimization_barrier(grain_force)[grain_keys].astype(jnp.float32)
    spread_force = jnp.einsum("zwx,znw->nzx", delta_weights, marker_pair_force, precision=lax.Precision.HIGHEST)
    spread_force = spread_force.reshape(3, pair_total, BX, BZ, BY)
    forced_velocity = predicted + jnp.zeros_like(predicted).at[:, cell_x, cell_z, cell_y].add(spread_force)
    forced_padded = extend(forced_velocity)
    divergence = along_x(forced_padded[0]) + along_y(forced_velocity[1]) + along_z(forced_padded[2])
    pressure = old_pressure
    for sweep in range(SWEEPS):
        pressure = (neighbours(extend(pressure)) - divergence) / 6.0
    new_velocity = forced_velocity - gradient_of(extend(pressure))
    return new_velocity, pressure
```

```python
import jax
import jax.numpy as jnp
from jax import lax
from jax.sharding import PartitionSpec as P

BX = 4
BZ = 4
BY = 8
S = 4


step_size = 0.1
viscosity = 1.5


def faces(block, axis, dim):
    count = lax.axis_size(axis)
    forward = [(i, (i + 1) % count) for i in range(count)]
    backward = [(target, source) for source, target in forward]
    low = lax.ppermute(
        lax.slice_in_dim(block, block.shape[dim] - 1, None, axis=dim), axis, forward
    )
    high = lax.ppermute(lax.slice_in_dim(block, 0, 1, axis=dim), axis, backward)
    return low, high


def padded_of(block, x_dim, z_dim, x_faces=None, z_faces=None):
    if x_faces is None:
        x_faces = faces(block, "gx", x_dim)
    if z_faces is None:
        z_faces = faces(block, "yz", z_dim)
    tile_index = lax.axis_index("yz")
    tile_total = lax.axis_size("yz")
    low_z, high_z = z_faces
    low_z = jnp.where(tile_index == 0, jnp.zeros_like(low_z), low_z)
    high_z = jnp.where(tile_index == tile_total - 1, jnp.zeros_like(high_z), high_z)
    middle = jnp.concatenate([low_z, block, high_z], axis=z_dim)
    pad_widths = [(0, 0)] * block.ndim
    pad_widths[z_dim] = (1, 1)
    low_x = jnp.pad(x_faces[0], pad_widths)
    high_x = jnp.pad(x_faces[1], pad_widths)
    return jnp.concatenate([low_x, middle, high_x], axis=x_dim)


def inner(padded):
    return padded[..., 1:-1, 1:-1, :]


def along_x(padded):
    return 0.5 * (padded[..., 2:, 1:-1, :] - padded[..., :-2, 1:-1, :])


def along_z(padded):
    return 0.5 * (padded[..., 1:-1, 2:, :] - padded[..., 1:-1, :-2, :])


def along_y(field):
    return 0.5 * (jnp.roll(field, -1, -1) - jnp.roll(field, 1, -1))


def neighbours(padded):
    middle = inner(padded)
    total = padded[..., 2:, 1:-1, :] + padded[..., :-2, 1:-1, :]
    total = total + padded[..., 1:-1, 2:, :] + padded[..., 1:-1, :-2, :]
    return total + jnp.roll(middle, 1, -1) + jnp.roll(middle, -1, -1)


def gradient_of(padded):
    middle = inner(padded)
    return jnp.stack([along_x(padded), along_y(middle), along_z(padded)])


def predict(flow_padded):
    velocity_padded = flow_padded[:3]
    pressure_padded = flow_padded[3]
    current = inner(velocity_padded)
    laplace = neighbours(velocity_padded) - 6.0 * current
    advect = current[0] * along_x(velocity_padded)
    return current + step_size * (viscosity * laplace - advect) - gradient_of(pressure_padded)


def body(velocity, old_pressure, delta_weight, marker_target, pair_owner, pair_grain, box_anchor):
    fields, cx, cz, ny = velocity.shape
    flow_fields = jnp.concatenate([velocity, old_pressure[None]], 0)
    flow_padded = padded_of(flow_fields, 1, 2)
    predicted = predict(flow_padded)

    anchors = box_anchor[0]
    owners = pair_owner[0, :, 0]
    grains = pair_grain[0]
    delta_weights = delta_weight[0]
    pair_total = anchors.shape[0]
    grain_slots = marker_target.shape[1]
    tiles = lax.axis_size("yz")
    box_rows = BX * BZ
    row_total = cx * cz

    steps = jnp.arange(box_rows, dtype=jnp.int32)
    rows_of = (anchors[:, 0, None] + steps[None, :] // BZ) * cz + anchors[:, 1, None] + steps[None, :] % BZ
    row_select = (
        rows_of.reshape(-1)[:, None] == jnp.arange(row_total, dtype=jnp.int32)[None, :]
    )
    lanes = jnp.arange(ny, dtype=jnp.int32)
    y_select = (
        lanes[None, :, None] == anchors[:, 2, None, None] + jnp.arange(BY, dtype=jnp.int32)[None, None, :]
    )

    predicted_rows = predicted.astype(jnp.bfloat16).reshape(fields, row_total, ny)
    box_lines = jnp.einsum(
        "qr,cry->qcy",
        row_select.astype(jnp.bfloat16),
        predicted_rows,
        preferred_element_type=jnp.float32,
    ).astype(jnp.bfloat16)
    box_lines = box_lines.reshape(pair_total, box_rows, fields, ny)
    kernel_box_values = jnp.einsum(
        "pkcy,pyj->pckj", box_lines, y_select.astype(jnp.bfloat16), preferred_element_type=jnp.float32
    ).astype(jnp.bfloat16).reshape(pair_total, fields, -1)
    partial_force_value = jnp.einsum(
        "pmb,pcb->pcm", delta_weights, kernel_box_values, preferred_element_type=jnp.float32
    )
    row_width = fields * partial_force_value.shape[2]
    flat_partial = partial_force_value.reshape(pair_total, row_width)

    same_owner = owners[:, None] == owners[None, :]
    earlier = jnp.arange(pair_total)[None, :] < jnp.arange(pair_total)[:, None]
    slots = jnp.sum(jnp.logical_and(same_owner, earlier), axis=1).astype(jnp.int32)
    places = owners * S + slots
    dispatch = (jnp.arange(tiles * S, dtype=jnp.int32)[:, None] == places[None, :]).astype(jnp.float32)
    packed = jnp.concatenate(
        [flat_partial, (grains + 1).astype(jnp.float32)[:, None]], axis=1
    )
    send = jnp.dot(
        dispatch, packed, precision=lax.Precision.HIGHEST, preferred_element_type=jnp.float32
    )
    received = lax.all_to_all(send, "yz", 0, 0, tiled=True)
    received_grain = received[:, row_width]
    received_values = received[:, :row_width]
    slot_numbers = jnp.arange(grain_slots, dtype=jnp.float32) + 1.0
    select = (slot_numbers[:, None] == received_grain[None, :]).astype(jnp.float32)
    summed = jnp.dot(
        select, received_values, precision=lax.Precision.HIGHEST, preferred_element_type=jnp.float32
    )
    targets = marker_target[0].reshape(grain_slots, row_width)
    grain_force = (targets - summed).astype(jnp.bfloat16)
    returned = jnp.einsum(
        "gq,gw->qw", select.astype(jnp.bfloat16), grain_force, preferred_element_type=jnp.float32
    ).astype(jnp.bfloat16)
    back = lax.all_to_all(returned, "yz", 0, 0, tiled=True)
    marker_pair_force = jnp.einsum(
        "qr,qw->rw", dispatch.astype(jnp.bfloat16), back, preferred_element_type=jnp.float32
    ).astype(jnp.bfloat16)

    spread_force = jnp.einsum(
        "pmb,pcm->pcb",
        delta_weights,
        marker_pair_force.reshape(pair_total, fields, -1),
        preferred_element_type=jnp.float32,
    )
    spread_lines = jnp.einsum(
        "pckj,pyj->pkcy",
        spread_force.reshape(pair_total, fields, box_rows, BY),
        y_select.astype(jnp.float32),
        precision=lax.Precision.HIGHEST,
        preferred_element_type=jnp.float32,
    ).reshape(pair_total * box_rows, fields, ny)
    added = jnp.einsum(
        "qr,qcy->cry",
        row_select.astype(jnp.float32),
        spread_lines,
        precision=lax.Precision.HIGHEST,
        preferred_element_type=jnp.float32,
    )
    forced_velocity = predicted + added.reshape(fields, cx, cz, ny)

    forced_x = padded_of(forced_velocity[0], 0, 1, z_faces=(jnp.zeros((cx, 1, ny), jnp.float32),) * 2)
    forced_z = padded_of(forced_velocity[2], 0, 1, x_faces=(jnp.zeros((1, cz, ny), jnp.float32),) * 2)
    divergence = along_x(forced_x) + along_y(forced_velocity[1]) + along_z(forced_z)
    pressure = (neighbours(flow_padded[3]) - divergence) / 6.0
    pressure = (neighbours(padded_of(pressure, 0, 1)) - divergence) / 6.0
    new_velocity = forced_velocity - gradient_of(padded_of(pressure, 0, 1))
    return (new_velocity, pressure)


def solution(mesh):
    placed = (
        P(None, "gx", "yz", None),
        P("gx", "yz", None),
        P("gx", "yz", None, None),
        P("gx", "yz", None, None),
        P("gx", "yz", None),
        P("gx", "yz"),
        P("gx", "yz", None),
    )
    return jax.shard_map(
        body,
        mesh=mesh,
        in_specs=placed,
        out_specs=(P(None, "gx", "yz", None), P("gx", "yz", None)),
        check_vma=False,
    )
```

```python
import jax
import jax.numpy as jnp
from jax import lax
from jax.sharding import PartitionSpec as P

BX = 4
BZ = 4
BY = 8
S = 4


step_size = 0.1
viscosity = 1.5


def faces(block, axis, dim):
    count = lax.axis_size(axis)
    forward = [(i, (i + 1) % count) for i in range(count)]
    backward = [(target, source) for source, target in forward]
    low = lax.ppermute(
        lax.slice_in_dim(block, block.shape[dim] - 1, None, axis=dim), axis, forward
    )
    high = lax.ppermute(lax.slice_in_dim(block, 0, 1, axis=dim), axis, backward)
    return low, high


def padded_of(block, x_dim, z_dim, x_faces=None, z_faces=None):
    if x_faces is None:
        x_faces = faces(block, "gx", x_dim)
    if z_faces is None:
        z_faces = faces(block, "yz", z_dim)
    tile_index = lax.axis_index("yz")
    tile_total = lax.axis_size("yz")
    low_z, high_z = z_faces
    low_z = jnp.where(tile_index == 0, jnp.zeros_like(low_z), low_z)
    high_z = jnp.where(tile_index == tile_total - 1, jnp.zeros_like(high_z), high_z)
    middle = jnp.concatenate([low_z, block, high_z], axis=z_dim)
    pad_widths = [(0, 0)] * block.ndim
    pad_widths[z_dim] = (1, 1)
    low_x = jnp.pad(x_faces[0], pad_widths)
    high_x = jnp.pad(x_faces[1], pad_widths)
    return jnp.concatenate([low_x, middle, high_x], axis=x_dim)


def inner(padded):
    return padded[..., 1:-1, 1:-1, :]


def along_x(padded):
    return 0.5 * (padded[..., 2:, 1:-1, :] - padded[..., :-2, 1:-1, :])


def along_z(padded):
    return 0.5 * (padded[..., 1:-1, 2:, :] - padded[..., 1:-1, :-2, :])


def along_y(field):
    return 0.5 * (jnp.roll(field, -1, -1) - jnp.roll(field, 1, -1))


def neighbours(padded):
    middle = inner(padded)
    total = padded[..., 2:, 1:-1, :] + padded[..., :-2, 1:-1, :]
    total = total + padded[..., 1:-1, 2:, :] + padded[..., 1:-1, :-2, :]
    return total + jnp.roll(middle, 1, -1) + jnp.roll(middle, -1, -1)


def gradient_of(padded):
    middle = inner(padded)
    return jnp.stack([along_x(padded), along_y(middle), along_z(padded)])


def predict(flow_padded):
    velocity_padded = flow_padded[:3]
    pressure_padded = flow_padded[3]
    current = inner(velocity_padded)
    laplace = neighbours(velocity_padded) - 6.0 * current
    advect = current[0] * along_x(velocity_padded)
    return current + step_size * (viscosity * laplace - advect) - gradient_of(pressure_padded)


def body(velocity, old_pressure, delta_weight, marker_target, pair_owner, pair_grain, box_anchor):
    fields, cx, cz, ny = velocity.shape
    flow_fields = jnp.concatenate([velocity, old_pressure[None]], 0)
    flow_padded = padded_of(flow_fields, 1, 2)
    predicted = predict(flow_padded)

    anchors = box_anchor[0]
    owners = pair_owner[0, :, 0]
    grains = pair_grain[0]
    delta_weights = delta_weight[0]
    pair_total = anchors.shape[0]
    grain_slots = marker_target.shape[1]
    tiles = lax.axis_size("yz")
    box_rows = BX * BZ
    row_total = cx * cz

    steps = jnp.arange(box_rows, dtype=jnp.int32)
    rows_of = (anchors[:, 0, None] + steps[None, :] // BZ) * cz + anchors[:, 1, None] + steps[None, :] % BZ
    row_select = (
        rows_of.reshape(-1)[:, None] == jnp.arange(row_total, dtype=jnp.int32)[None, :]
    )
    lanes = jnp.arange(ny, dtype=jnp.int32)

    predicted_rows = predicted.astype(jnp.bfloat16).reshape(fields, row_total, ny)
    row_pick = row_select.astype(jnp.bfloat16)
    box_lines = jnp.stack(
        [
            jnp.dot(row_pick, predicted_rows[c], preferred_element_type=jnp.float32)
            for c in range(fields)
        ]
    )
    line_offset = jnp.repeat(anchors[:, 2], box_rows)[:, None]
    window = jnp.stack(
        [jnp.sum(jnp.where(lanes[None, None, :] == line_offset + j, box_lines, 0.0), axis=-1) for j in range(BY)],
        axis=-1,
    )
    kernel_box_values = (
        window.reshape(fields, pair_total, box_rows * BY).transpose(1, 0, 2).astype(jnp.bfloat16)
    )
    partial_force_value = jnp.einsum(
        "pmb,pcb->pcm", delta_weights, kernel_box_values, preferred_element_type=jnp.float32
    )
    row_width = fields * partial_force_value.shape[2]
    flat_partial = partial_force_value.reshape(pair_total, row_width)

    same_owner = owners[:, None] == owners[None, :]
    earlier = jnp.arange(pair_total)[None, :] < jnp.arange(pair_total)[:, None]
    slots = jnp.sum(jnp.logical_and(same_owner, earlier), axis=1).astype(jnp.int32)
    places = owners * S + slots
    dispatch = (jnp.arange(tiles * S, dtype=jnp.int32)[:, None] == places[None, :]).astype(jnp.float32)
    packed = jnp.concatenate(
        [flat_partial, (grains + 1).astype(jnp.float32)[:, None]], axis=1
    )
    send = jnp.dot(
        dispatch, packed, precision=lax.Precision.HIGHEST, preferred_element_type=jnp.float32
    )
    received = lax.all_to_all(send, "yz", 0, 0, tiled=True)
    received_grain = received[:, row_width]
    received_values = received[:, :row_width]
    slot_numbers = jnp.arange(grain_slots, dtype=jnp.float32) + 1.0
    select = (slot_numbers[:, None] == received_grain[None, :]).astype(jnp.float32)
    summed = jnp.dot(
        select, received_values, precision=lax.Precision.HIGHEST, preferred_element_type=jnp.float32
    )
    targets = marker_target[0].reshape(grain_slots, row_width)
    grain_force = (targets - summed).astype(jnp.bfloat16)
    returned = jnp.einsum(
        "gq,gw->qw", select.astype(jnp.bfloat16), grain_force, preferred_element_type=jnp.float32
    ).astype(jnp.bfloat16)
    back = lax.all_to_all(returned, "yz", 0, 0, tiled=True)
    marker_pair_force = jnp.einsum(
        "qr,qw->rw", dispatch.astype(jnp.bfloat16), back, preferred_element_type=jnp.float32
    ).astype(jnp.bfloat16)

    spread_force = jnp.einsum(
        "pmb,pcm->pcb",
        delta_weights,
        marker_pair_force.reshape(pair_total, fields, -1),
        preferred_element_type=jnp.float32,
    )
    spread_window = spread_force.transpose(1, 0, 2).reshape(fields, pair_total * box_rows, BY)
    spread_lines = sum(
        jnp.where(lanes[None, None, :] == line_offset + j, spread_window[:, :, j, None], 0.0)
        for j in range(BY)
    )
    row_place = (
        jnp.arange(row_total, dtype=jnp.int32)[:, None] == rows_of.reshape(-1)[None, :]
    ).astype(jnp.float32)
    added = jnp.stack(
        [
            jnp.dot(
                row_place,
                spread_lines[c],
                precision=lax.Precision.HIGHEST,
                preferred_element_type=jnp.float32,
            )
            for c in range(fields)
        ]
    )
    forced_velocity = predicted + added.reshape(fields, cx, cz, ny)

    forced_x = padded_of(forced_velocity[0], 0, 1, z_faces=(jnp.zeros((cx, 1, ny), jnp.float32),) * 2)
    forced_z = padded_of(forced_velocity[2], 0, 1, x_faces=(jnp.zeros((1, cz, ny), jnp.float32),) * 2)
    divergence = along_x(forced_x) + along_y(forced_velocity[1]) + along_z(forced_z)
    pressure = (neighbours(flow_padded[3]) - divergence) / 6.0
    pressure = (neighbours(padded_of(pressure, 0, 1)) - divergence) / 6.0
    new_velocity = forced_velocity - gradient_of(padded_of(pressure, 0, 1))
    return (new_velocity, pressure)


def solution(mesh):
    placed = (
        P(None, "gx", "yz", None),
        P("gx", "yz", None),
        P("gx", "yz", None, None),
        P("gx", "yz", None, None),
        P("gx", "yz", None),
        P("gx", "yz"),
        P("gx", "yz", None),
    )
    return jax.shard_map(
        body,
        mesh=mesh,
        in_specs=placed,
        out_specs=(P(None, "gx", "yz", None), P("gx", "yz", None)),
        check_vma=False,
    )
```

```python
import jax
import jax.numpy as jnp
from jax import lax
from jax.sharding import PartitionSpec as P

BX = 4
BZ = 4
BY = 8
S = 4


step_size = 0.1
viscosity = 1.5


def faces(block, axis, dim):
    count = lax.axis_size(axis)
    forward = [(i, (i + 1) % count) for i in range(count)]
    backward = [(target, source) for source, target in forward]
    low = lax.ppermute(
        lax.slice_in_dim(block, block.shape[dim] - 1, None, axis=dim), axis, forward
    )
    high = lax.ppermute(lax.slice_in_dim(block, 0, 1, axis=dim), axis, backward)
    return low, high


def padded_of(block, x_dim, z_dim, x_faces=None, z_faces=None):
    if x_faces is None:
        x_faces = faces(block, "gx", x_dim)
    if z_faces is None:
        z_faces = faces(block, "yz", z_dim)
    tile_index = lax.axis_index("yz")
    tile_total = lax.axis_size("yz")
    low_z, high_z = z_faces
    low_z = jnp.where(tile_index == 0, jnp.zeros_like(low_z), low_z)
    high_z = jnp.where(tile_index == tile_total - 1, jnp.zeros_like(high_z), high_z)
    middle = jnp.concatenate([low_z, block, high_z], axis=z_dim)
    pad_widths = [(0, 0)] * block.ndim
    pad_widths[z_dim] = (1, 1)
    low_x = jnp.pad(x_faces[0], pad_widths)
    high_x = jnp.pad(x_faces[1], pad_widths)
    return jnp.concatenate([low_x, middle, high_x], axis=x_dim)


def halo(block, width):
    x_count = lax.axis_size("gx")
    z_count = lax.axis_size("yz")
    x_total, z_total = block.shape[-3], block.shape[-2]

    def sent(piece, dx, dz):
        if dz == 0:
            pairs = [(i, (i + dx) % x_count) for i in range(x_count)]
            return lax.ppermute(piece, "gx", pairs)
        if dx == 0:
            pairs = [(t, (t + dz) % z_count) for t in range(z_count)]
            return lax.ppermute(piece, "yz", pairs)
        pairs = [
            (i * z_count + t, ((i + dx) % x_count) * z_count + (t + dz) % z_count)
            for i in range(x_count)
            for t in range(z_count)
        ]
        return lax.ppermute(piece, ("gx", "yz"), pairs)

    top_x = slice(x_total - width, None)
    low_x = slice(0, width)
    top_z = slice(z_total - width, None)
    low_z = slice(0, width)
    every = slice(None)
    lead = (Ellipsis,)
    below = jnp.concatenate(
        [
            sent(block[lead + (top_x, top_z, every)], 1, 1),
            sent(block[lead + (top_x, every, every)], 1, 0),
            sent(block[lead + (top_x, low_z, every)], 1, -1),
        ],
        axis=-2,
    )
    middle = jnp.concatenate(
        [sent(block[lead + (every, top_z, every)], 0, 1), block, sent(block[lead + (every, low_z, every)], 0, -1)],
        axis=-2,
    )
    above = jnp.concatenate(
        [
            sent(block[lead + (low_x, top_z, every)], -1, 1),
            sent(block[lead + (low_x, every, every)], -1, 0),
            sent(block[lead + (low_x, low_z, every)], -1, -1),
        ],
        axis=-2,
    )
    return inside(jnp.concatenate([below, middle, above], axis=-3), width, z_total)


def inside(field, width, z_total):
    tile_index = lax.axis_index("yz")
    z_count = lax.axis_size("yz")
    position = lax.broadcasted_iota(jnp.int32, field.shape, field.ndim - 2) + tile_index * z_total - width
    valid = jnp.logical_and(position >= 0, position < z_count * z_total)
    return jnp.where(valid, field, jnp.zeros((), field.dtype))


def inner(padded):
    return padded[..., 1:-1, 1:-1, :]


def along_x(padded):
    return 0.5 * (padded[..., 2:, 1:-1, :] - padded[..., :-2, 1:-1, :])


def along_z(padded):
    return 0.5 * (padded[..., 1:-1, 2:, :] - padded[..., 1:-1, :-2, :])


def along_y(field):
    return 0.5 * (jnp.roll(field, -1, -1) - jnp.roll(field, 1, -1))


def neighbours(padded):
    middle = inner(padded)
    total = padded[..., 2:, 1:-1, :] + padded[..., :-2, 1:-1, :]
    total = total + padded[..., 1:-1, 2:, :] + padded[..., 1:-1, :-2, :]
    return total + jnp.roll(middle, 1, -1) + jnp.roll(middle, -1, -1)


def gradient_of(padded):
    middle = inner(padded)
    return jnp.stack([along_x(padded), along_y(middle), along_z(padded)])


def predict(flow_padded):
    velocity_padded = flow_padded[:3]
    pressure_padded = flow_padded[3]
    current = inner(velocity_padded)
    laplace = neighbours(velocity_padded) - 6.0 * current
    advect = current[0] * along_x(velocity_padded)
    return current + step_size * (viscosity * laplace - advect) - gradient_of(pressure_padded)


def body(velocity, old_pressure, delta_weight, marker_target, pair_owner, pair_grain, box_anchor):
    fields, cx, cz, ny = velocity.shape
    flow_fields = jnp.concatenate([velocity, old_pressure[None]], 0)
    reach = 3
    flow_wide = halo(flow_fields, reach + 1)
    predicted_wide = predict(flow_wide)
    predicted = predicted_wide[:, reach:-reach, reach:-reach, :]

    anchors = box_anchor[0]
    owners = pair_owner[0, :, 0]
    grains = pair_grain[0]
    delta_weights = delta_weight[0]
    pair_total = anchors.shape[0]
    grain_slots = marker_target.shape[1]
    tiles = lax.axis_size("yz")
    box_rows = BX * BZ
    row_total = cx * cz

    steps = jnp.arange(box_rows, dtype=jnp.int32)
    rows_of = (anchors[:, 0, None] + steps[None, :] // BZ) * cz + anchors[:, 1, None] + steps[None, :] % BZ
    row_select = (
        rows_of.reshape(-1)[:, None] == jnp.arange(row_total, dtype=jnp.int32)[None, :]
    )
    lanes = jnp.arange(ny, dtype=jnp.int32)

    predicted_rows = predicted.astype(jnp.bfloat16).reshape(fields, row_total, ny)
    row_pick = row_select.astype(jnp.bfloat16)
    box_lines = jnp.stack(
        [
            jnp.dot(row_pick, predicted_rows[c], preferred_element_type=jnp.float32)
            for c in range(fields)
        ]
    )
    line_offset = jnp.repeat(anchors[:, 2], box_rows)[:, None]
    window = jnp.stack(
        [jnp.sum(jnp.where(lanes[None, None, :] == line_offset + j, box_lines, 0.0), axis=-1) for j in range(BY)],
        axis=-1,
    )
    kernel_box_values = (
        window.reshape(fields, pair_total, box_rows * BY).transpose(1, 0, 2).astype(jnp.bfloat16)
    )
    partial_force_value = jnp.einsum(
        "pmb,pcb->pcm", delta_weights, kernel_box_values, preferred_element_type=jnp.float32
    )
    row_width = fields * partial_force_value.shape[2]
    flat_partial = partial_force_value.reshape(pair_total, row_width)

    same_owner = owners[:, None] == owners[None, :]
    earlier = jnp.arange(pair_total)[None, :] < jnp.arange(pair_total)[:, None]
    slots = jnp.sum(jnp.logical_and(same_owner, earlier), axis=1).astype(jnp.int32)
    places = owners * S + slots
    dispatch = (jnp.arange(tiles * S, dtype=jnp.int32)[:, None] == places[None, :]).astype(jnp.float32)
    packed = jnp.concatenate(
        [flat_partial, (grains + 1).astype(jnp.float32)[:, None]], axis=1
    )
    send = jnp.dot(
        dispatch, packed, precision=lax.Precision.HIGHEST, preferred_element_type=jnp.float32
    )
    received = lax.all_to_all(send, "yz", 0, 0, tiled=True)
    received_grain = received[:, row_width]
    received_values = received[:, :row_width]
    slot_numbers = jnp.arange(grain_slots, dtype=jnp.float32) + 1.0
    select = (slot_numbers[:, None] == received_grain[None, :]).astype(jnp.float32)
    summed = jnp.dot(
        select, received_values, precision=lax.Precision.HIGHEST, preferred_element_type=jnp.float32
    )
    targets = marker_target[0].reshape(grain_slots, row_width)
    grain_force = (targets - summed).astype(jnp.bfloat16)
    returned = jnp.einsum(
        "gq,gw->qw", select.astype(jnp.bfloat16), grain_force, preferred_element_type=jnp.float32
    ).astype(jnp.bfloat16)
    back = lax.all_to_all(returned, "yz", 0, 0, tiled=True)
    marker_pair_force = jnp.einsum(
        "qr,qw->rw", dispatch.astype(jnp.bfloat16), back, preferred_element_type=jnp.float32
    ).astype(jnp.bfloat16)

    spread_force = jnp.einsum(
        "pmb,pcm->pcb",
        delta_weights,
        marker_pair_force.reshape(pair_total, fields, -1),
        preferred_element_type=jnp.float32,
    )
    spread_window = spread_force.transpose(1, 0, 2).reshape(fields, pair_total * box_rows, BY)
    spread_lines = sum(
        jnp.where(lanes[None, None, :] == line_offset + j, spread_window[:, :, j, None], 0.0)
        for j in range(BY)
    )
    row_place = (
        jnp.arange(row_total, dtype=jnp.int32)[:, None] == rows_of.reshape(-1)[None, :]
    ).astype(jnp.float32)
    added = jnp.stack(
        [
            jnp.dot(
                row_place,
                spread_lines[c],
                precision=lax.Precision.HIGHEST,
                preferred_element_type=jnp.float32,
            )
            for c in range(fields)
        ]
    )
    added = added.reshape(fields, cx, cz, ny)
    forced_wide = inside(predicted_wide + halo(added, reach), reach, cz)
    divergence = (
        along_x(forced_wide[0]) + along_y(inner(forced_wide[1])) + along_z(forced_wide[2])
    )
    pressure = inside((neighbours(inner(flow_wide[3])) - divergence) / 6.0, reach - 1, cz)
    pressure = inside((neighbours(pressure) - inner(divergence)) / 6.0, reach - 2, cz)
    new_velocity = forced_wide[:, reach:-reach, reach:-reach, :] - gradient_of(pressure)
    pressure = inner(pressure)
    return (new_velocity, pressure)


def solution(mesh):
    placed = (
        P(None, "gx", "yz", None),
        P("gx", "yz", None),
        P("gx", "yz", None, None),
        P("gx", "yz", None, None),
        P("gx", "yz", None),
        P("gx", "yz"),
        P("gx", "yz", None),
    )
    return jax.shard_map(
        body,
        mesh=mesh,
        in_specs=placed,
        out_specs=(P(None, "gx", "yz", None), P("gx", "yz", None)),
        check_vma=False,
    )
```

```python
import jax
import jax.numpy as jnp
from jax import lax
from jax.sharding import PartitionSpec as P

BX = 4
BZ = 4
BY = 8
S = 4


step_size = 0.1
viscosity = 1.5


def faces(block, axis, dim):
    count = lax.axis_size(axis)
    forward = [(i, (i + 1) % count) for i in range(count)]
    backward = [(target, source) for source, target in forward]
    low = lax.ppermute(
        lax.slice_in_dim(block, block.shape[dim] - 1, None, axis=dim), axis, forward
    )
    high = lax.ppermute(lax.slice_in_dim(block, 0, 1, axis=dim), axis, backward)
    return low, high


def padded_of(block, x_dim, z_dim, x_faces=None, z_faces=None):
    if x_faces is None:
        x_faces = faces(block, "gx", x_dim)
    if z_faces is None:
        z_faces = faces(block, "yz", z_dim)
    tile_index = lax.axis_index("yz")
    tile_total = lax.axis_size("yz")
    low_z, high_z = z_faces
    low_z = jnp.where(tile_index == 0, jnp.zeros_like(low_z), low_z)
    high_z = jnp.where(tile_index == tile_total - 1, jnp.zeros_like(high_z), high_z)
    middle = jnp.concatenate([low_z, block, high_z], axis=z_dim)
    pad_widths = [(0, 0)] * block.ndim
    pad_widths[z_dim] = (1, 1)
    low_x = jnp.pad(x_faces[0], pad_widths)
    high_x = jnp.pad(x_faces[1], pad_widths)
    return jnp.concatenate([low_x, middle, high_x], axis=x_dim)


def inner(padded):
    return padded[..., 1:-1, 1:-1, :]


def along_x(padded):
    return 0.5 * (padded[..., 2:, 1:-1, :] - padded[..., :-2, 1:-1, :])


def along_z(padded):
    return 0.5 * (padded[..., 1:-1, 2:, :] - padded[..., 1:-1, :-2, :])


def along_y(field):
    return 0.5 * (jnp.roll(field, -1, -1) - jnp.roll(field, 1, -1))


def neighbours(padded):
    middle = inner(padded)
    total = padded[..., 2:, 1:-1, :] + padded[..., :-2, 1:-1, :]
    total = total + padded[..., 1:-1, 2:, :] + padded[..., 1:-1, :-2, :]
    return total + jnp.roll(middle, 1, -1) + jnp.roll(middle, -1, -1)


def gradient_of(padded):
    middle = inner(padded)
    return jnp.stack([along_x(padded), along_y(middle), along_z(padded)])


def predict(flow_padded):
    velocity_padded = flow_padded[:3]
    pressure_padded = flow_padded[3]
    current = inner(velocity_padded)
    laplace = neighbours(velocity_padded) - 6.0 * current
    advect = current[0] * along_x(velocity_padded)
    return current + step_size * (viscosity * laplace - advect) - gradient_of(pressure_padded)


def body(velocity, old_pressure, delta_weight, marker_target, pair_owner, pair_grain, box_anchor):
    fields, cx, cz, ny = velocity.shape
    flow_fields = jnp.concatenate([velocity, old_pressure[None]], 0)
    flow_padded = padded_of(flow_fields, 1, 2)
    predicted = predict(flow_padded)

    anchors = box_anchor[0]
    owners = pair_owner[0, :, 0]
    grains = pair_grain[0]
    delta_weights = delta_weight[0]
    pair_total = anchors.shape[0]
    grain_slots = marker_target.shape[1]
    tiles = lax.axis_size("yz")
    box_rows = BX * BZ
    row_total = cx * cz

    steps = jnp.arange(box_rows, dtype=jnp.int32)
    rows_of = (anchors[:, 0, None] + steps[None, :] // BZ) * cz + anchors[:, 1, None] + steps[None, :] % BZ
    row_select = (
        rows_of.reshape(-1)[:, None] == jnp.arange(row_total, dtype=jnp.int32)[None, :]
    )
    lanes = jnp.arange(ny, dtype=jnp.int32)

    predicted_rows = predicted.astype(jnp.bfloat16).reshape(fields, row_total, ny)
    row_pick = row_select.astype(jnp.bfloat16)
    box_lines = jnp.stack(
        [
            jnp.dot(row_pick, predicted_rows[c], preferred_element_type=jnp.float32)
            for c in range(fields)
        ]
    )
    line_offset = jnp.repeat(anchors[:, 2], box_rows)[:, None]
    window = jnp.stack(
        [jnp.sum(jnp.where(lanes[None, None, :] == line_offset + j, box_lines, 0.0), axis=-1) for j in range(BY)],
        axis=-1,
    )
    kernel_box_values = (
        window.reshape(fields, pair_total, box_rows * BY).transpose(1, 0, 2).astype(jnp.bfloat16)
    )
    partial_force_value = jnp.einsum(
        "pmb,pcb->pcm", delta_weights, kernel_box_values, preferred_element_type=jnp.float32
    )
    row_width = fields * partial_force_value.shape[2]
    flat_partial = partial_force_value.reshape(pair_total, row_width)

    same_owner = owners[:, None] == owners[None, :]
    earlier = jnp.arange(pair_total)[None, :] < jnp.arange(pair_total)[:, None]
    slots = jnp.sum(jnp.logical_and(same_owner, earlier), axis=1).astype(jnp.int32)
    places = owners * S + slots
    dispatch = (jnp.arange(tiles * S, dtype=jnp.int32)[:, None] == places[None, :]).astype(jnp.float32)
    send = jnp.dot(
        dispatch, flat_partial, precision=lax.Precision.HIGHEST, preferred_element_type=jnp.float32
    )
    send_grain = jnp.sum(
        jnp.where(dispatch > 0, (grains + 1)[None, :], 0), axis=1
    ).astype(jnp.int32)
    received_grain = lax.all_to_all(send_grain, "yz", 0, 0, tiled=True)
    received_values = lax.all_to_all(send, "yz", 0, 0, tiled=True)
    slot_numbers = jnp.arange(grain_slots, dtype=jnp.int32) + 1
    select = (slot_numbers[:, None] == received_grain[None, :]).astype(jnp.float32)
    summed = jnp.dot(
        select, received_values, precision=lax.Precision.HIGHEST, preferred_element_type=jnp.float32
    )
    targets = marker_target[0].reshape(grain_slots, row_width)
    grain_force = (targets - summed).astype(jnp.bfloat16)
    returned = jnp.einsum(
        "gq,gw->qw", select.astype(jnp.bfloat16), grain_force, preferred_element_type=jnp.float32
    ).astype(jnp.bfloat16)
    back = lax.all_to_all(returned, "yz", 0, 0, tiled=True)
    marker_pair_force = jnp.einsum(
        "qr,qw->rw", dispatch.astype(jnp.bfloat16), back, preferred_element_type=jnp.float32
    ).astype(jnp.bfloat16)

    spread_force = jnp.einsum(
        "pmb,pcm->pcb",
        delta_weights,
        marker_pair_force.reshape(pair_total, fields, -1),
        preferred_element_type=jnp.float32,
    )
    spread_window = spread_force.transpose(1, 0, 2).reshape(fields, pair_total * box_rows, BY)
    spread_lines = sum(
        jnp.where(lanes[None, None, :] == line_offset + j, spread_window[:, :, j, None], 0.0)
        for j in range(BY)
    )
    row_place = (
        jnp.arange(row_total, dtype=jnp.int32)[:, None] == rows_of.reshape(-1)[None, :]
    ).astype(jnp.float32)
    added = jnp.stack(
        [
            jnp.dot(
                row_place,
                spread_lines[c],
                precision=lax.Precision.HIGHEST,
                preferred_element_type=jnp.float32,
            )
            for c in range(fields)
        ]
    )
    forced_velocity = predicted + added.reshape(fields, cx, cz, ny)

    forced_x = padded_of(forced_velocity[0], 0, 1, z_faces=(jnp.zeros((cx, 1, ny), jnp.float32),) * 2)
    forced_z = padded_of(forced_velocity[2], 0, 1, x_faces=(jnp.zeros((1, cz, ny), jnp.float32),) * 2)
    divergence = along_x(forced_x) + along_y(forced_velocity[1]) + along_z(forced_z)
    pressure = (neighbours(flow_padded[3]) - divergence) / 6.0
    pressure = (neighbours(padded_of(pressure, 0, 1)) - divergence) / 6.0
    new_velocity = forced_velocity - gradient_of(padded_of(pressure, 0, 1))
    return (new_velocity, pressure)


def solution(mesh):
    placed = (
        P(None, "gx", "yz", None),
        P("gx", "yz", None),
        P("gx", "yz", None, None),
        P("gx", "yz", None, None),
        P("gx", "yz", None),
        P("gx", "yz"),
        P("gx", "yz", None),
    )
    return jax.shard_map(
        body,
        mesh=mesh,
        in_specs=placed,
        out_specs=(P(None, "gx", "yz", None), P("gx", "yz", None)),
        check_vma=False,
    )
```

```python
import jax
import jax.numpy as jnp
from jax import lax
from jax.sharding import PartitionSpec as P

BX = 4
BZ = 4
BY = 8
S = 4


step_size = 0.1
viscosity = 1.5


def faces(block, axis, dim, width=1):
    count = lax.axis_size(axis)
    forward = [(i, (i + 1) % count) for i in range(count)]
    backward = [(target, source) for source, target in forward]
    low = lax.ppermute(
        lax.slice_in_dim(block, block.shape[dim] - width, None, axis=dim), axis, forward
    )
    high = lax.ppermute(lax.slice_in_dim(block, 0, width, axis=dim), axis, backward)
    return low, high


def padded_of(block, x_dim, z_dim, x_faces=None, z_faces=None):
    if x_faces is None:
        x_faces = faces(block, "gx", x_dim)
    if z_faces is None:
        z_faces = faces(block, "yz", z_dim)
    tile_index = lax.axis_index("yz")
    tile_total = lax.axis_size("yz")
    low_z, high_z = z_faces
    low_z = jnp.where(tile_index == 0, jnp.zeros_like(low_z), low_z)
    high_z = jnp.where(tile_index == tile_total - 1, jnp.zeros_like(high_z), high_z)
    middle = jnp.concatenate([low_z, block, high_z], axis=z_dim)
    pad_widths = [(0, 0)] * block.ndim
    pad_widths[z_dim] = (1, 1)
    low_x = jnp.pad(x_faces[0], pad_widths)
    high_x = jnp.pad(x_faces[1], pad_widths)
    return jnp.concatenate([low_x, middle, high_x], axis=x_dim)


def halo(block, width):
    x_total, z_total = block.shape[-3], block.shape[-2]
    low, high = faces(block, "gx", block.ndim - 3, width)
    grown = jnp.concatenate([low, block, high], axis=-3)
    low, high = faces(grown, "yz", block.ndim - 2, width)
    return inside(jnp.concatenate([low, grown, high], axis=-2), width, z_total)


def inside(field, width, z_total):
    tile_index = lax.axis_index("yz")
    z_count = lax.axis_size("yz")
    position = lax.broadcasted_iota(jnp.int32, field.shape, field.ndim - 2) + tile_index * z_total - width
    valid = jnp.logical_and(position >= 0, position < z_count * z_total)
    return jnp.where(valid, field, jnp.zeros((), field.dtype))


def inner(padded):
    return padded[..., 1:-1, 1:-1, :]


def along_x(padded):
    return 0.5 * (padded[..., 2:, 1:-1, :] - padded[..., :-2, 1:-1, :])


def along_z(padded):
    return 0.5 * (padded[..., 1:-1, 2:, :] - padded[..., 1:-1, :-2, :])


def along_y(field):
    return 0.5 * (jnp.roll(field, -1, -1) - jnp.roll(field, 1, -1))


def neighbours(padded):
    middle = inner(padded)
    total = padded[..., 2:, 1:-1, :] + padded[..., :-2, 1:-1, :]
    total = total + padded[..., 1:-1, 2:, :] + padded[..., 1:-1, :-2, :]
    return total + jnp.roll(middle, 1, -1) + jnp.roll(middle, -1, -1)


def gradient_of(padded):
    middle = inner(padded)
    return jnp.stack([along_x(padded), along_y(middle), along_z(padded)])


def predict(flow_padded):
    velocity_padded = flow_padded[:3]
    pressure_padded = flow_padded[3]
    current = inner(velocity_padded)
    laplace = neighbours(velocity_padded) - 6.0 * current
    advect = current[0] * along_x(velocity_padded)
    return current + step_size * (viscosity * laplace - advect) - gradient_of(pressure_padded)


def body(velocity, old_pressure, delta_weight, marker_target, pair_owner, pair_grain, box_anchor):
    fields, cx, cz, ny = velocity.shape
    flow_fields = jnp.concatenate([velocity, old_pressure[None]], 0)
    flow_padded = padded_of(flow_fields, 1, 2)
    predicted = predict(flow_padded)
    reach = 3
    pressure_wide = halo(old_pressure, reach)

    anchors = box_anchor[0]
    owners = pair_owner[0, :, 0]
    grains = pair_grain[0]
    delta_weights = delta_weight[0]
    pair_total = anchors.shape[0]
    grain_slots = marker_target.shape[1]
    tiles = lax.axis_size("yz")
    box_rows = BX * BZ
    row_total = cx * cz

    steps = jnp.arange(box_rows, dtype=jnp.int32)
    rows_of = (anchors[:, 0, None] + steps[None, :] // BZ) * cz + anchors[:, 1, None] + steps[None, :] % BZ
    row_select = (
        rows_of.reshape(-1)[:, None] == jnp.arange(row_total, dtype=jnp.int32)[None, :]
    )
    lanes = jnp.arange(ny, dtype=jnp.int32)

    predicted_rows = predicted.astype(jnp.bfloat16).reshape(fields, row_total, ny)
    row_pick = row_select.astype(jnp.bfloat16)
    box_lines = jnp.stack(
        [
            jnp.dot(row_pick, predicted_rows[c], preferred_element_type=jnp.float32)
            for c in range(fields)
        ]
    )
    line_offset = jnp.repeat(anchors[:, 2], box_rows)[:, None]
    window = jnp.stack(
        [jnp.sum(jnp.where(lanes[None, None, :] == line_offset + j, box_lines, 0.0), axis=-1) for j in range(BY)],
        axis=-1,
    )
    kernel_box_values = (
        window.reshape(fields, pair_total, box_rows * BY).transpose(1, 0, 2).astype(jnp.bfloat16)
    )
    partial_force_value = jnp.einsum(
        "pmb,pcb->pcm", delta_weights, kernel_box_values, preferred_element_type=jnp.float32
    )
    row_width = fields * partial_force_value.shape[2]
    flat_partial = partial_force_value.reshape(pair_total, row_width)

    same_owner = owners[:, None] == owners[None, :]
    earlier = jnp.arange(pair_total)[None, :] < jnp.arange(pair_total)[:, None]
    slots = jnp.sum(jnp.logical_and(same_owner, earlier), axis=1).astype(jnp.int32)
    places = owners * S + slots
    dispatch = (jnp.arange(tiles * S, dtype=jnp.int32)[:, None] == places[None, :]).astype(jnp.float32)
    packed = jnp.concatenate(
        [flat_partial, (grains + 1).astype(jnp.float32)[:, None]], axis=1
    )
    send = jnp.dot(
        dispatch, packed, precision=lax.Precision.HIGHEST, preferred_element_type=jnp.float32
    )
    received = lax.all_to_all(send, "yz", 0, 0, tiled=True)
    received_grain = received[:, row_width]
    received_values = received[:, :row_width]
    slot_numbers = jnp.arange(grain_slots, dtype=jnp.float32) + 1.0
    select = (slot_numbers[:, None] == received_grain[None, :]).astype(jnp.float32)
    summed = jnp.dot(
        select, received_values, precision=lax.Precision.HIGHEST, preferred_element_type=jnp.float32
    )
    targets = marker_target[0].reshape(grain_slots, row_width)
    grain_force = (targets - summed).astype(jnp.bfloat16)
    returned = jnp.einsum(
        "gq,gw->qw", select.astype(jnp.bfloat16), grain_force, preferred_element_type=jnp.float32
    ).astype(jnp.bfloat16)
    back = lax.all_to_all(returned, "yz", 0, 0, tiled=True)
    marker_pair_force = jnp.einsum(
        "qr,qw->rw", dispatch.astype(jnp.bfloat16), back, preferred_element_type=jnp.float32
    ).astype(jnp.bfloat16)

    spread_force = jnp.einsum(
        "pmb,pcm->pcb",
        delta_weights,
        marker_pair_force.reshape(pair_total, fields, -1),
        preferred_element_type=jnp.float32,
    )
    spread_window = spread_force.transpose(1, 0, 2).reshape(fields, pair_total * box_rows, BY)
    spread_lines = sum(
        jnp.where(lanes[None, None, :] == line_offset + j, spread_window[:, :, j, None], 0.0)
        for j in range(BY)
    )
    row_place = (
        jnp.arange(row_total, dtype=jnp.int32)[:, None] == rows_of.reshape(-1)[None, :]
    ).astype(jnp.float32)
    added = jnp.stack(
        [
            jnp.dot(
                row_place,
                spread_lines[c],
                precision=lax.Precision.HIGHEST,
                preferred_element_type=jnp.float32,
            )
            for c in range(fields)
        ]
    )
    forced_velocity = predicted + added.reshape(fields, cx, cz, ny)

    forced_wide = halo(forced_velocity, reach)
    divergence = (
        along_x(forced_wide[0]) + along_y(inner(forced_wide[1])) + along_z(forced_wide[2])
    )
    pressure = inside((neighbours(pressure_wide) - divergence) / 6.0, reach - 1, cz)
    pressure = inside((neighbours(pressure) - inner(divergence)) / 6.0, reach - 2, cz)
    new_velocity = forced_velocity - gradient_of(pressure)
    pressure = inner(pressure)
    return (new_velocity, pressure)


def solution(mesh):
    placed = (
        P(None, "gx", "yz", None),
        P("gx", "yz", None),
        P("gx", "yz", None, None),
        P("gx", "yz", None, None),
        P("gx", "yz", None),
        P("gx", "yz"),
        P("gx", "yz", None),
    )
    return jax.shard_map(
        body,
        mesh=mesh,
        in_specs=placed,
        out_specs=(P(None, "gx", "yz", None), P("gx", "yz", None)),
        check_vma=False,
    )
```

```python
import jax
import jax.numpy as jnp
from jax import lax
from jax.sharding import PartitionSpec as P

BX = 4
BZ = 4
BY = 8
S = 4


step_size = 0.1
viscosity = 1.5


def faces(block, axis, dim, width=1):
    count = lax.axis_size(axis)
    forward = [(i, (i + 1) % count) for i in range(count)]
    backward = [(target, source) for source, target in forward]
    low = lax.ppermute(
        lax.slice_in_dim(block, block.shape[dim] - width, None, axis=dim), axis, forward
    )
    high = lax.ppermute(lax.slice_in_dim(block, 0, width, axis=dim), axis, backward)
    return low, high


def padded_of(block, x_dim, z_dim, x_faces=None, z_faces=None):
    if x_faces is None:
        x_faces = faces(block, "gx", x_dim)
    if z_faces is None:
        z_faces = faces(block, "yz", z_dim)
    tile_index = lax.axis_index("yz")
    tile_total = lax.axis_size("yz")
    low_z, high_z = z_faces
    low_z = jnp.where(tile_index == 0, jnp.zeros_like(low_z), low_z)
    high_z = jnp.where(tile_index == tile_total - 1, jnp.zeros_like(high_z), high_z)
    middle = jnp.concatenate([low_z, block, high_z], axis=z_dim)
    pad_widths = [(0, 0)] * block.ndim
    pad_widths[z_dim] = (1, 1)
    low_x = jnp.pad(x_faces[0], pad_widths)
    high_x = jnp.pad(x_faces[1], pad_widths)
    return jnp.concatenate([low_x, middle, high_x], axis=x_dim)


def halo(block, width, x_faces=None):
    x_total, z_total = block.shape[-3], block.shape[-2]
    low, high = x_faces if x_faces is not None else faces(block, "gx", block.ndim - 3, width)
    grown = jnp.concatenate([low, block, high], axis=-3)
    low, high = faces(grown, "yz", block.ndim - 2, width)
    return inside(jnp.concatenate([low, grown, high], axis=-2), width, z_total)


def inside(field, width, z_total):
    tile_index = lax.axis_index("yz")
    z_count = lax.axis_size("yz")
    position = lax.broadcasted_iota(jnp.int32, field.shape, field.ndim - 2) + tile_index * z_total - width
    valid = jnp.logical_and(position >= 0, position < z_count * z_total)
    return jnp.where(valid, field, jnp.zeros((), field.dtype))


def inner(padded):
    return padded[..., 1:-1, 1:-1, :]


def along_x(padded):
    return 0.5 * (padded[..., 2:, 1:-1, :] - padded[..., :-2, 1:-1, :])


def along_z(padded):
    return 0.5 * (padded[..., 1:-1, 2:, :] - padded[..., 1:-1, :-2, :])


def along_y(field):
    return 0.5 * (jnp.roll(field, -1, -1) - jnp.roll(field, 1, -1))


def neighbours(padded):
    middle = inner(padded)
    total = padded[..., 2:, 1:-1, :] + padded[..., :-2, 1:-1, :]
    total = total + padded[..., 1:-1, 2:, :] + padded[..., 1:-1, :-2, :]
    return total + jnp.roll(middle, 1, -1) + jnp.roll(middle, -1, -1)


def gradient_of(padded):
    middle = inner(padded)
    return jnp.stack([along_x(padded), along_y(middle), along_z(padded)])


def predict(flow_padded):
    velocity_padded = flow_padded[:3]
    pressure_padded = flow_padded[3]
    current = inner(velocity_padded)
    laplace = neighbours(velocity_padded) - 6.0 * current
    advect = current[0] * along_x(velocity_padded)
    return current + step_size * (viscosity * laplace - advect) - gradient_of(pressure_padded)


def body(velocity, old_pressure, delta_weight, marker_target, pair_owner, pair_grain, box_anchor):
    fields, cx, cz, ny = velocity.shape
    flow_fields = jnp.concatenate([velocity, old_pressure[None]], 0)
    reach = 3
    low_x, high_x = faces(flow_fields, "gx", 1, reach)
    flow_padded = padded_of(flow_fields, 1, 2, x_faces=(low_x[:, reach - 1 :], high_x[:, :1]))
    predicted = predict(flow_padded)
    pressure_wide = halo(old_pressure, reach, x_faces=(low_x[fields], high_x[fields]))

    anchors = box_anchor[0]
    owners = pair_owner[0, :, 0]
    grains = pair_grain[0]
    delta_weights = delta_weight[0]
    pair_total = anchors.shape[0]
    grain_slots = marker_target.shape[1]
    tiles = lax.axis_size("yz")
    box_rows = BX * BZ
    row_total = cx * cz

    steps = jnp.arange(box_rows, dtype=jnp.int32)
    rows_of = (anchors[:, 0, None] + steps[None, :] // BZ) * cz + anchors[:, 1, None] + steps[None, :] % BZ
    row_select = (
        rows_of.reshape(-1)[:, None] == jnp.arange(row_total, dtype=jnp.int32)[None, :]
    )
    lanes = jnp.arange(ny, dtype=jnp.int32)

    predicted_rows = predicted.astype(jnp.bfloat16).reshape(fields, row_total, ny)
    row_pick = row_select.astype(jnp.bfloat16)
    box_lines = jnp.stack(
        [
            jnp.dot(row_pick, predicted_rows[c], preferred_element_type=jnp.float32)
            for c in range(fields)
        ]
    )
    line_offset = jnp.repeat(anchors[:, 2], box_rows)[:, None]
    window = jnp.stack(
        [jnp.sum(jnp.where(lanes[None, None, :] == line_offset + j, box_lines, 0.0), axis=-1) for j in range(BY)],
        axis=-1,
    )
    kernel_box_values = (
        window.reshape(fields, pair_total, box_rows * BY).transpose(1, 0, 2).astype(jnp.bfloat16)
    )
    partial_force_value = jnp.einsum(
        "pmb,pcb->pcm", delta_weights, kernel_box_values, preferred_element_type=jnp.float32
    )
    row_width = fields * partial_force_value.shape[2]
    flat_partial = partial_force_value.reshape(pair_total, row_width)

    same_owner = owners[:, None] == owners[None, :]
    earlier = jnp.arange(pair_total)[None, :] < jnp.arange(pair_total)[:, None]
    slots = jnp.sum(jnp.logical_and(same_owner, earlier), axis=1).astype(jnp.int32)
    places = owners * S + slots
    dispatch = (jnp.arange(tiles * S, dtype=jnp.int32)[:, None] == places[None, :]).astype(jnp.float32)
    packed = jnp.concatenate(
        [flat_partial, (grains + 1).astype(jnp.float32)[:, None]], axis=1
    )
    send = jnp.dot(
        dispatch, packed, precision=lax.Precision.HIGHEST, preferred_element_type=jnp.float32
    )
    received = lax.all_to_all(send, "yz", 0, 0, tiled=True)
    received_grain = received[:, row_width]
    received_values = received[:, :row_width]
    slot_numbers = jnp.arange(grain_slots, dtype=jnp.float32) + 1.0
    select = (slot_numbers[:, None] == received_grain[None, :]).astype(jnp.float32)
    summed = jnp.dot(
        select, received_values, precision=lax.Precision.HIGHEST, preferred_element_type=jnp.float32
    )
    targets = marker_target[0].reshape(grain_slots, row_width)
    grain_force = (targets - summed).astype(jnp.bfloat16)
    returned = jnp.einsum(
        "gq,gw->qw", select.astype(jnp.bfloat16), grain_force, preferred_element_type=jnp.float32
    ).astype(jnp.bfloat16)
    back = lax.all_to_all(returned, "yz", 0, 0, tiled=True)
    marker_pair_force = jnp.einsum(
        "qr,qw->rw", dispatch.astype(jnp.bfloat16), back, preferred_element_type=jnp.float32
    ).astype(jnp.bfloat16)

    spread_force = jnp.einsum(
        "pmb,pcm->pcb",
        delta_weights,
        marker_pair_force.reshape(pair_total, fields, -1),
        preferred_element_type=jnp.float32,
    )
    spread_window = spread_force.transpose(1, 0, 2).reshape(fields, pair_total * box_rows, BY)
    spread_lines = sum(
        jnp.where(lanes[None, None, :] == line_offset + j, spread_window[:, :, j, None], 0.0)
        for j in range(BY)
    )
    row_place = (
        jnp.arange(row_total, dtype=jnp.int32)[:, None] == rows_of.reshape(-1)[None, :]
    ).astype(jnp.float32)
    added = jnp.stack(
        [
            jnp.dot(
                row_place,
                spread_lines[c],
                precision=lax.Precision.HIGHEST,
                preferred_element_type=jnp.float32,
            )
            for c in range(fields)
        ]
    )
    forced_velocity = predicted + added.reshape(fields, cx, cz, ny)

    forced_wide = halo(forced_velocity, reach)
    divergence = (
        along_x(forced_wide[0]) + along_y(inner(forced_wide[1])) + along_z(forced_wide[2])
    )
    pressure = inside((neighbours(pressure_wide) - divergence) / 6.0, reach - 1, cz)
    pressure = inside((neighbours(pressure) - inner(divergence)) / 6.0, reach - 2, cz)
    new_velocity = forced_velocity - gradient_of(pressure)
    pressure = inner(pressure)
    return (new_velocity, pressure)


def solution(mesh):
    placed = (
        P(None, "gx", "yz", None),
        P("gx", "yz", None),
        P("gx", "yz", None, None),
        P("gx", "yz", None, None),
        P("gx", "yz", None),
        P("gx", "yz"),
        P("gx", "yz", None),
    )
    return jax.shard_map(
        body,
        mesh=mesh,
        in_specs=placed,
        out_specs=(P(None, "gx", "yz", None), P("gx", "yz", None)),
        check_vma=False,
    )
```

```python
import jax
import jax.numpy as jnp
from jax import lax
from jax.sharding import PartitionSpec as P

BX = 4
BZ = 4
BY = 8
S = 4


step_size = 0.1
viscosity = 1.5


def faces(block, axis, dim, width=1, carried=None):
    count = lax.axis_size(axis)
    forward = [(i, (i + 1) % count) for i in range(count)]
    backward = [(target, source) for source, target in forward]
    kind = carried or block.dtype
    low = lax.ppermute(
        lax.slice_in_dim(block, block.shape[dim] - width, None, axis=dim).astype(kind), axis, forward
    )
    high = lax.ppermute(lax.slice_in_dim(block, 0, width, axis=dim).astype(kind), axis, backward)
    return low.astype(block.dtype), high.astype(block.dtype)


def padded_of(block, x_dim, z_dim, x_faces=None, z_faces=None):
    if x_faces is None:
        x_faces = faces(block, "gx", x_dim)
    if z_faces is None:
        z_faces = faces(block, "yz", z_dim)
    tile_index = lax.axis_index("yz")
    tile_total = lax.axis_size("yz")
    low_z, high_z = z_faces
    low_z = jnp.where(tile_index == 0, jnp.zeros_like(low_z), low_z)
    high_z = jnp.where(tile_index == tile_total - 1, jnp.zeros_like(high_z), high_z)
    middle = jnp.concatenate([low_z, block, high_z], axis=z_dim)
    pad_widths = [(0, 0)] * block.ndim
    pad_widths[z_dim] = (1, 1)
    low_x = jnp.pad(x_faces[0], pad_widths)
    high_x = jnp.pad(x_faces[1], pad_widths)
    return jnp.concatenate([low_x, middle, high_x], axis=x_dim)


def halo(block, width, x_faces=None, carried=None):
    x_total, z_total = block.shape[-3], block.shape[-2]
    low, high = x_faces if x_faces is not None else faces(block, "gx", block.ndim - 3, width, carried)
    grown = jnp.concatenate([low, block, high], axis=-3)
    low, high = faces(grown, "yz", block.ndim - 2, width, carried)
    return inside(jnp.concatenate([low, grown, high], axis=-2), width, z_total)


def inside(field, width, z_total):
    tile_index = lax.axis_index("yz")
    z_count = lax.axis_size("yz")
    position = lax.broadcasted_iota(jnp.int32, field.shape, field.ndim - 2) + tile_index * z_total - width
    valid = jnp.logical_and(position >= 0, position < z_count * z_total)
    return jnp.where(valid, field, jnp.zeros((), field.dtype))


def inner(padded):
    return padded[..., 1:-1, 1:-1, :]


def along_x(padded):
    return 0.5 * (padded[..., 2:, 1:-1, :] - padded[..., :-2, 1:-1, :])


def along_z(padded):
    return 0.5 * (padded[..., 1:-1, 2:, :] - padded[..., 1:-1, :-2, :])


def along_y(field):
    return 0.5 * (jnp.roll(field, -1, -1) - jnp.roll(field, 1, -1))


def neighbours(padded):
    middle = inner(padded)
    total = padded[..., 2:, 1:-1, :] + padded[..., :-2, 1:-1, :]
    total = total + padded[..., 1:-1, 2:, :] + padded[..., 1:-1, :-2, :]
    return total + jnp.roll(middle, 1, -1) + jnp.roll(middle, -1, -1)


def gradient_of(padded):
    middle = inner(padded)
    return jnp.stack([along_x(padded), along_y(middle), along_z(padded)])


def predict(flow_padded):
    velocity_padded = flow_padded[:3]
    pressure_padded = flow_padded[3]
    current = inner(velocity_padded)
    laplace = neighbours(velocity_padded) - 6.0 * current
    advect = current[0] * along_x(velocity_padded)
    return current + step_size * (viscosity * laplace - advect) - gradient_of(pressure_padded)


def body(velocity, old_pressure, delta_weight, marker_target, pair_owner, pair_grain, box_anchor):
    fields, cx, cz, ny = velocity.shape
    flow_fields = jnp.concatenate([velocity, old_pressure[None]], 0)
    reach = 3
    low_x, high_x = faces(flow_fields, "gx", 1, reach)
    flow_padded = padded_of(flow_fields, 1, 2, x_faces=(low_x[:, reach - 1 :], high_x[:, :1]))
    predicted = predict(flow_padded)
    pressure_wide = halo(old_pressure, reach, x_faces=(low_x[fields], high_x[fields]))

    anchors = box_anchor[0]
    owners = pair_owner[0, :, 0]
    grains = pair_grain[0]
    delta_weights = delta_weight[0]
    pair_total = anchors.shape[0]
    grain_slots = marker_target.shape[1]
    tiles = lax.axis_size("yz")
    box_rows = BX * BZ
    row_total = cx * cz

    steps = jnp.arange(box_rows, dtype=jnp.int32)
    rows_of = (anchors[:, 0, None] + steps[None, :] // BZ) * cz + anchors[:, 1, None] + steps[None, :] % BZ
    row_select = (
        rows_of.reshape(-1)[:, None] == jnp.arange(row_total, dtype=jnp.int32)[None, :]
    )
    lanes = jnp.arange(ny, dtype=jnp.int32)

    predicted_rows = predicted.astype(jnp.bfloat16).reshape(fields, row_total, ny)
    row_pick = row_select.astype(jnp.bfloat16)
    box_lines = jnp.stack(
        [
            jnp.dot(row_pick, predicted_rows[c], preferred_element_type=jnp.float32)
            for c in range(fields)
        ]
    )
    line_offset = jnp.repeat(anchors[:, 2], box_rows)[:, None]
    window = jnp.stack(
        [jnp.sum(jnp.where(lanes[None, None, :] == line_offset + j, box_lines, 0.0), axis=-1) for j in range(BY)],
        axis=-1,
    )
    kernel_box_values = (
        window.reshape(fields, pair_total, box_rows * BY).transpose(1, 0, 2).astype(jnp.bfloat16)
    )
    partial_force_value = jnp.einsum(
        "pmb,pcb->pcm", delta_weights, kernel_box_values, preferred_element_type=jnp.float32
    )
    row_width = fields * partial_force_value.shape[2]
    flat_partial = partial_force_value.reshape(pair_total, row_width)

    same_owner = owners[:, None] == owners[None, :]
    earlier = jnp.arange(pair_total)[None, :] < jnp.arange(pair_total)[:, None]
    slots = jnp.sum(jnp.logical_and(same_owner, earlier), axis=1).astype(jnp.int32)
    places = owners * S + slots
    dispatch = (jnp.arange(tiles * S, dtype=jnp.int32)[:, None] == places[None, :]).astype(jnp.float32)
    packed = jnp.concatenate(
        [flat_partial, (grains + 1).astype(jnp.float32)[:, None]], axis=1
    )
    send = jnp.dot(
        dispatch, packed, precision=lax.Precision.HIGHEST, preferred_element_type=jnp.float32
    )
    received = lax.all_to_all(send, "yz", 0, 0, tiled=True)
    received_grain = received[:, row_width]
    received_values = received[:, :row_width]
    slot_numbers = jnp.arange(grain_slots, dtype=jnp.float32) + 1.0
    select = (slot_numbers[:, None] == received_grain[None, :]).astype(jnp.float32)
    summed = jnp.dot(
        select, received_values, precision=lax.Precision.HIGHEST, preferred_element_type=jnp.float32
    )
    targets = marker_target[0].reshape(grain_slots, row_width)
    grain_force = (targets - summed).astype(jnp.bfloat16)
    returned = jnp.einsum(
        "gq,gw->qw", select.astype(jnp.bfloat16), grain_force, preferred_element_type=jnp.float32
    ).astype(jnp.bfloat16)
    back = lax.all_to_all(returned, "yz", 0, 0, tiled=True)
    marker_pair_force = jnp.einsum(
        "qr,qw->rw", dispatch.astype(jnp.bfloat16), back, preferred_element_type=jnp.float32
    ).astype(jnp.bfloat16)

    spread_force = jnp.einsum(
        "pmb,pcm->pcb",
        delta_weights,
        marker_pair_force.reshape(pair_total, fields, -1),
        preferred_element_type=jnp.float32,
    )
    spread_window = spread_force.transpose(1, 0, 2).reshape(fields, pair_total * box_rows, BY)
    spread_lines = sum(
        jnp.where(lanes[None, None, :] == line_offset + j, spread_window[:, :, j, None], 0.0)
        for j in range(BY)
    )
    row_place = (
        jnp.arange(row_total, dtype=jnp.int32)[:, None] == rows_of.reshape(-1)[None, :]
    ).astype(jnp.float32)
    added = jnp.stack(
        [
            jnp.dot(
                row_place,
                spread_lines[c],
                precision=lax.Precision.HIGHEST,
                preferred_element_type=jnp.float32,
            )
            for c in range(fields)
        ]
    )
    forced_velocity = predicted + added.reshape(fields, cx, cz, ny)

    forced_wide = halo(forced_velocity, reach, carried=jnp.bfloat16)
    divergence = (
        along_x(forced_wide[0]) + along_y(inner(forced_wide[1])) + along_z(forced_wide[2])
    )
    pressure = inside((neighbours(pressure_wide) - divergence) / 6.0, reach - 1, cz)
    pressure = inside((neighbours(pressure) - inner(divergence)) / 6.0, reach - 2, cz)
    new_velocity = forced_velocity - gradient_of(pressure)
    pressure = inner(pressure)
    return (new_velocity, pressure)


def solution(mesh):
    placed = (
        P(None, "gx", "yz", None),
        P("gx", "yz", None),
        P("gx", "yz", None, None),
        P("gx", "yz", None, None),
        P("gx", "yz", None),
        P("gx", "yz"),
        P("gx", "yz", None),
    )
    return jax.shard_map(
        body,
        mesh=mesh,
        in_specs=placed,
        out_specs=(P(None, "gx", "yz", None), P("gx", "yz", None)),
        check_vma=False,
    )
```

```python
import jax
import jax.numpy as jnp
from jax import lax
from jax.sharding import PartitionSpec as P

BX = 4
BZ = 4
BY = 8
S = 4


step_size = 0.1
viscosity = 1.5


def faces(block, axis, dim, width=1, carried=None):
    count = lax.axis_size(axis)
    forward = [(i, (i + 1) % count) for i in range(count)]
    backward = [(target, source) for source, target in forward]
    kind = carried or block.dtype
    low = lax.ppermute(
        lax.slice_in_dim(block, block.shape[dim] - width, None, axis=dim).astype(kind), axis, forward
    )
    high = lax.ppermute(lax.slice_in_dim(block, 0, width, axis=dim).astype(kind), axis, backward)
    return low.astype(block.dtype), high.astype(block.dtype)


def padded_of(block, x_dim, z_dim, x_faces=None, z_faces=None):
    if x_faces is None:
        x_faces = faces(block, "gx", x_dim)
    if z_faces is None:
        z_faces = faces(block, "yz", z_dim)
    tile_index = lax.axis_index("yz")
    tile_total = lax.axis_size("yz")
    low_z, high_z = z_faces
    low_z = jnp.where(tile_index == 0, jnp.zeros_like(low_z), low_z)
    high_z = jnp.where(tile_index == tile_total - 1, jnp.zeros_like(high_z), high_z)
    middle = jnp.concatenate([low_z, block, high_z], axis=z_dim)
    pad_widths = [(0, 0)] * block.ndim
    pad_widths[z_dim] = (1, 1)
    low_x = jnp.pad(x_faces[0], pad_widths)
    high_x = jnp.pad(x_faces[1], pad_widths)
    return jnp.concatenate([low_x, middle, high_x], axis=x_dim)


def halo(block, width, x_faces=None, carried=None):
    x_total, z_total = block.shape[-3], block.shape[-2]
    low, high = x_faces if x_faces is not None else faces(block, "gx", block.ndim - 3, width, carried)
    grown = jnp.concatenate([low, block, high], axis=-3)
    low, high = faces(grown, "yz", block.ndim - 2, width, carried)
    return inside(jnp.concatenate([low, grown, high], axis=-2), width, z_total)


def inside(field, width, z_total):
    tile_index = lax.axis_index("yz")
    z_count = lax.axis_size("yz")
    position = lax.broadcasted_iota(jnp.int32, field.shape, field.ndim - 2) + tile_index * z_total - width
    valid = jnp.logical_and(position >= 0, position < z_count * z_total)
    return jnp.where(valid, field, jnp.zeros((), field.dtype))


def inner(padded):
    return padded[..., 1:-1, 1:-1, :]


def along_x(padded):
    return 0.5 * (padded[..., 2:, 1:-1, :] - padded[..., :-2, 1:-1, :])


def along_z(padded):
    return 0.5 * (padded[..., 1:-1, 2:, :] - padded[..., 1:-1, :-2, :])


def across_y(field, weights):
    size = field.shape[-1]
    source = lax.broadcasted_iota(jnp.int32, (size, size), 0)
    target = lax.broadcasted_iota(jnp.int32, (size, size), 1)
    above = (source == (target + 1) % size).astype(jnp.float32)
    below = (source == (target + size - 1) % size).astype(jnp.float32)
    matrix = weights[0] * above + weights[1] * below
    return jnp.einsum(
        "...i,ij->...j", field, matrix, precision=lax.Precision.HIGHEST, preferred_element_type=jnp.float32
    )


def along_y(field):
    return across_y(field, (0.5, -0.5))


def neighbours(padded):
    middle = inner(padded)
    total = padded[..., 2:, 1:-1, :] + padded[..., :-2, 1:-1, :]
    total = total + padded[..., 1:-1, 2:, :] + padded[..., 1:-1, :-2, :]
    return total + across_y(middle, (1.0, 1.0))


def gradient_of(padded):
    middle = inner(padded)
    return jnp.stack([along_x(padded), along_y(middle), along_z(padded)])


def predict(flow_padded):
    velocity_padded = flow_padded[:3]
    pressure_padded = flow_padded[3]
    current = inner(velocity_padded)
    laplace = neighbours(velocity_padded) - 6.0 * current
    advect = current[0] * along_x(velocity_padded)
    return current + step_size * (viscosity * laplace - advect) - gradient_of(pressure_padded)


def body(velocity, old_pressure, delta_weight, marker_target, pair_owner, pair_grain, box_anchor):
    fields, cx, cz, ny = velocity.shape
    flow_fields = jnp.concatenate([velocity, old_pressure[None]], 0)
    reach = 3
    low_x, high_x = faces(flow_fields, "gx", 1, reach)
    flow_padded = padded_of(flow_fields, 1, 2, x_faces=(low_x[:, reach - 1 :], high_x[:, :1]))
    predicted = predict(flow_padded)
    pressure_wide = halo(old_pressure, reach, x_faces=(low_x[fields], high_x[fields]))

    anchors = box_anchor[0]
    owners = pair_owner[0, :, 0]
    grains = pair_grain[0]
    delta_weights = delta_weight[0]
    pair_total = anchors.shape[0]
    grain_slots = marker_target.shape[1]
    tiles = lax.axis_size("yz")
    box_rows = BX * BZ
    row_total = cx * cz

    steps = jnp.arange(box_rows, dtype=jnp.int32)
    rows_of = (anchors[:, 0, None] + steps[None, :] // BZ) * cz + anchors[:, 1, None] + steps[None, :] % BZ
    row_select = (
        rows_of.reshape(-1)[:, None] == jnp.arange(row_total, dtype=jnp.int32)[None, :]
    )
    lanes = jnp.arange(ny, dtype=jnp.int32)

    predicted_rows = predicted.astype(jnp.bfloat16).reshape(fields, row_total, ny)
    row_pick = row_select.astype(jnp.bfloat16)
    box_lines = jnp.stack(
        [
            jnp.dot(row_pick, predicted_rows[c], preferred_element_type=jnp.float32)
            for c in range(fields)
        ]
    )
    line_offset = jnp.repeat(anchors[:, 2], box_rows)[:, None]
    window = jnp.stack(
        [jnp.sum(jnp.where(lanes[None, None, :] == line_offset + j, box_lines, 0.0), axis=-1) for j in range(BY)],
        axis=-1,
    )
    kernel_box_values = (
        window.reshape(fields, pair_total, box_rows * BY).transpose(1, 0, 2).astype(jnp.bfloat16)
    )
    partial_force_value = jnp.einsum(
        "pmb,pcb->pcm", delta_weights, kernel_box_values, preferred_element_type=jnp.float32
    )
    row_width = fields * partial_force_value.shape[2]
    flat_partial = partial_force_value.reshape(pair_total, row_width)

    same_owner = owners[:, None] == owners[None, :]
    earlier = jnp.arange(pair_total)[None, :] < jnp.arange(pair_total)[:, None]
    slots = jnp.sum(jnp.logical_and(same_owner, earlier), axis=1).astype(jnp.int32)
    places = owners * S + slots
    dispatch = (jnp.arange(tiles * S, dtype=jnp.int32)[:, None] == places[None, :]).astype(jnp.float32)
    packed = jnp.concatenate(
        [flat_partial, (grains + 1).astype(jnp.float32)[:, None]], axis=1
    )
    send = jnp.dot(
        dispatch, packed, precision=lax.Precision.HIGHEST, preferred_element_type=jnp.float32
    )
    received = lax.all_to_all(send, "yz", 0, 0, tiled=True)
    received_grain = received[:, row_width]
    received_values = received[:, :row_width]
    slot_numbers = jnp.arange(grain_slots, dtype=jnp.float32) + 1.0
    select = (slot_numbers[:, None] == received_grain[None, :]).astype(jnp.float32)
    summed = jnp.dot(
        select, received_values, precision=lax.Precision.HIGHEST, preferred_element_type=jnp.float32
    )
    targets = marker_target[0].reshape(grain_slots, row_width)
    grain_force = (targets - summed).astype(jnp.bfloat16)
    returned = jnp.einsum(
        "gq,gw->qw", select.astype(jnp.bfloat16), grain_force, preferred_element_type=jnp.float32
    ).astype(jnp.bfloat16)
    back = lax.all_to_all(returned, "yz", 0, 0, tiled=True)
    marker_pair_force = jnp.einsum(
        "qr,qw->rw", dispatch.astype(jnp.bfloat16), back, preferred_element_type=jnp.float32
    ).astype(jnp.bfloat16)

    spread_force = jnp.einsum(
        "pmb,pcm->pcb",
        delta_weights,
        marker_pair_force.reshape(pair_total, fields, -1),
        preferred_element_type=jnp.float32,
    )
    spread_window = spread_force.transpose(1, 0, 2).reshape(fields, pair_total * box_rows, BY)
    spread_lines = sum(
        jnp.where(lanes[None, None, :] == line_offset + j, spread_window[:, :, j, None], 0.0)
        for j in range(BY)
    )
    row_place = (
        jnp.arange(row_total, dtype=jnp.int32)[:, None] == rows_of.reshape(-1)[None, :]
    ).astype(jnp.float32)
    added = jnp.stack(
        [
            jnp.dot(
                row_place,
                spread_lines[c],
                precision=lax.Precision.HIGHEST,
                preferred_element_type=jnp.float32,
            )
            for c in range(fields)
        ]
    )
    forced_velocity = predicted + added.reshape(fields, cx, cz, ny)

    forced_wide = halo(forced_velocity, reach, carried=jnp.bfloat16)
    divergence = (
        along_x(forced_wide[0]) + along_y(inner(forced_wide[1])) + along_z(forced_wide[2])
    )
    pressure = inside((neighbours(pressure_wide) - divergence) / 6.0, reach - 1, cz)
    pressure = inside((neighbours(pressure) - inner(divergence)) / 6.0, reach - 2, cz)
    new_velocity = forced_velocity - gradient_of(pressure)
    pressure = inner(pressure)
    return (new_velocity, pressure)


def solution(mesh):
    placed = (
        P(None, "gx", "yz", None),
        P("gx", "yz", None),
        P("gx", "yz", None, None),
        P("gx", "yz", None, None),
        P("gx", "yz", None),
        P("gx", "yz"),
        P("gx", "yz", None),
    )
    return jax.shard_map(
        body,
        mesh=mesh,
        in_specs=placed,
        out_specs=(P(None, "gx", "yz", None), P("gx", "yz", None)),
        check_vma=False,
    )
```

```python
import jax
import jax.numpy as jnp
from jax import lax
from jax.sharding import PartitionSpec as P

BX = 4
BZ = 4
BY = 8
S = 4


step_size = 0.1
viscosity = 1.5


def faces(block, axis, dim, width=1, carried=None):
    count = lax.axis_size(axis)
    forward = [(i, (i + 1) % count) for i in range(count)]
    backward = [(target, source) for source, target in forward]
    kind = carried or block.dtype
    low = lax.ppermute(
        lax.slice_in_dim(block, block.shape[dim] - width, None, axis=dim).astype(kind), axis, forward
    )
    high = lax.ppermute(lax.slice_in_dim(block, 0, width, axis=dim).astype(kind), axis, backward)
    return low.astype(block.dtype), high.astype(block.dtype)


def padded_of(block, x_dim, z_dim, x_faces=None, z_faces=None):
    if x_faces is None:
        x_faces = faces(block, "gx", x_dim)
    if z_faces is None:
        z_faces = faces(block, "yz", z_dim)
    tile_index = lax.axis_index("yz")
    tile_total = lax.axis_size("yz")
    low_z, high_z = z_faces
    low_z = jnp.where(tile_index == 0, jnp.zeros_like(low_z), low_z)
    high_z = jnp.where(tile_index == tile_total - 1, jnp.zeros_like(high_z), high_z)
    middle = jnp.concatenate([low_z, block, high_z], axis=z_dim)
    pad_widths = [(0, 0)] * block.ndim
    pad_widths[z_dim] = (1, 1)
    low_x = jnp.pad(x_faces[0], pad_widths)
    high_x = jnp.pad(x_faces[1], pad_widths)
    return jnp.concatenate([low_x, middle, high_x], axis=x_dim)


def halo(block, width, x_faces=None, carried=None):
    x_total, z_total = block.shape[-3], block.shape[-2]
    low, high = x_faces if x_faces is not None else faces(block, "gx", block.ndim - 3, width, carried)
    grown = jnp.concatenate([low, block, high], axis=-3)
    low, high = faces(grown, "yz", block.ndim - 2, width, carried)
    return inside(jnp.concatenate([low, grown, high], axis=-2), width, z_total)


def inside(field, width, z_total):
    tile_index = lax.axis_index("yz")
    z_count = lax.axis_size("yz")
    position = lax.broadcasted_iota(jnp.int32, field.shape, field.ndim - 2) + tile_index * z_total - width
    valid = jnp.logical_and(position >= 0, position < z_count * z_total)
    return jnp.where(valid, field, jnp.zeros((), field.dtype))


def inner(padded):
    return padded[..., 1:-1, 1:-1, :]


def along_x(padded):
    return 0.5 * (padded[..., 2:, 1:-1, :] - padded[..., :-2, 1:-1, :])


def along_z(padded):
    return 0.5 * (padded[..., 1:-1, 2:, :] - padded[..., 1:-1, :-2, :])


def across_y(field, weights):
    size = field.shape[-1]
    source = lax.broadcasted_iota(jnp.int32, (size, size), 0)
    target = lax.broadcasted_iota(jnp.int32, (size, size), 1)
    above = (source == (target + 1) % size).astype(jnp.float32)
    below = (source == (target + size - 1) % size).astype(jnp.float32)
    matrix = weights[0] * above + weights[1] * below
    return jnp.einsum(
        "...i,ij->...j", field, matrix, precision=lax.Precision.HIGHEST, preferred_element_type=jnp.float32
    )


def along_y(field):
    return across_y(field, (0.5, -0.5))


def neighbours(padded):
    middle = inner(padded)
    total = padded[..., 2:, 1:-1, :] + padded[..., :-2, 1:-1, :]
    total = total + padded[..., 1:-1, 2:, :] + padded[..., 1:-1, :-2, :]
    return total + across_y(middle, (1.0, 1.0))


def gradient_of(padded):
    middle = inner(padded)
    return jnp.stack([along_x(padded), along_y(middle), along_z(padded)])


def predict(flow_padded):
    velocity_padded = flow_padded[:3]
    pressure_padded = flow_padded[3]
    current = inner(velocity_padded)
    laplace = neighbours(velocity_padded) - 6.0 * current
    advect = current[0] * along_x(velocity_padded)
    return current + step_size * (viscosity * laplace - advect) - gradient_of(pressure_padded)


def body(velocity, old_pressure, delta_weight, marker_target, pair_owner, pair_grain, box_anchor):
    fields, cx, cz, ny = velocity.shape
    flow_fields = jnp.concatenate([velocity, old_pressure[None]], 0)
    reach = 3
    low_x, high_x = faces(flow_fields, "gx", 1, reach)
    flow_padded = padded_of(flow_fields, 1, 2, x_faces=(low_x[:, reach - 1 :], high_x[:, :1]))
    predicted = predict(flow_padded)
    pressure_wide = halo(old_pressure, reach, x_faces=(low_x[fields], high_x[fields]))

    anchors = box_anchor[0]
    owners = pair_owner[0, :, 0]
    grains = pair_grain[0]
    delta_weights = delta_weight[0]
    pair_total = anchors.shape[0]
    grain_slots = marker_target.shape[1]
    tiles = lax.axis_size("yz")
    box_rows = BX * BZ
    row_total = cx * cz

    steps = jnp.arange(box_rows, dtype=jnp.int32)
    rows_of = (anchors[:, 0, None] + steps[None, :] // BZ) * cz + anchors[:, 1, None] + steps[None, :] % BZ
    row_select = (
        rows_of.reshape(-1)[:, None] == jnp.arange(row_total, dtype=jnp.int32)[None, :]
    )
    lanes = jnp.arange(ny, dtype=jnp.int32)

    predicted_rows = predicted.astype(jnp.bfloat16).reshape(fields, row_total, ny)
    row_pick = row_select.astype(jnp.bfloat16)
    box_lines = jnp.stack(
        [
            jnp.dot(row_pick, predicted_rows[c], preferred_element_type=jnp.float32)
            for c in range(fields)
        ]
    )
    line_offset = jnp.repeat(anchors[:, 2], box_rows)[:, None]
    window = jnp.stack(
        [jnp.sum(jnp.where(lanes[None, None, :] == line_offset + j, box_lines, 0.0), axis=-1) for j in range(BY)],
        axis=-1,
    )
    kernel_box_values = (
        window.reshape(fields, pair_total, box_rows * BY).transpose(1, 0, 2).astype(jnp.bfloat16)
    )
    partial_force_value = jnp.einsum(
        "pmb,pcb->pcm", delta_weights, kernel_box_values, preferred_element_type=jnp.float32
    )
    row_width = fields * partial_force_value.shape[2]
    flat_partial = partial_force_value.reshape(pair_total, row_width)

    same_owner = owners[:, None] == owners[None, :]
    earlier = jnp.arange(pair_total)[None, :] < jnp.arange(pair_total)[:, None]
    slots = jnp.sum(jnp.logical_and(same_owner, earlier), axis=1).astype(jnp.int32)
    places = owners * S + slots
    dispatch = (jnp.arange(tiles * S, dtype=jnp.int32)[:, None] == places[None, :]).astype(jnp.float32)
    packed = jnp.concatenate(
        [flat_partial, (grains + 1).astype(jnp.float32)[:, None]], axis=1
    )
    send = jnp.dot(
        dispatch, packed, precision=lax.Precision.HIGHEST, preferred_element_type=jnp.float32
    )
    received = lax.all_to_all(send, "yz", 0, 0, tiled=True)
    received_grain = received[:, row_width]
    received_values = received[:, :row_width]
    slot_numbers = jnp.arange(grain_slots, dtype=jnp.float32) + 1.0
    select = (slot_numbers[:, None] == received_grain[None, :]).astype(jnp.float32)
    summed = jnp.dot(
        select, received_values, precision=lax.Precision.HIGHEST, preferred_element_type=jnp.float32
    )
    targets = marker_target[0].reshape(grain_slots, row_width)
    grain_force = (targets - summed).astype(jnp.bfloat16)
    returned = jnp.einsum(
        "gq,gw->qw", select.astype(jnp.bfloat16), grain_force, preferred_element_type=jnp.float32
    ).astype(jnp.bfloat16)
    pressure_wide, returned = lax.optimization_barrier((pressure_wide, returned))
    back = lax.all_to_all(returned, "yz", 0, 0, tiled=True)
    marker_pair_force = jnp.einsum(
        "qr,qw->rw", dispatch.astype(jnp.bfloat16), back, preferred_element_type=jnp.float32
    ).astype(jnp.bfloat16)

    spread_force = jnp.einsum(
        "pmb,pcm->pcb",
        delta_weights,
        marker_pair_force.reshape(pair_total, fields, -1),
        preferred_element_type=jnp.float32,
    )
    spread_window = spread_force.transpose(1, 0, 2).reshape(fields, pair_total * box_rows, BY)
    spread_lines = sum(
        jnp.where(lanes[None, None, :] == line_offset + j, spread_window[:, :, j, None], 0.0)
        for j in range(BY)
    )
    row_place = (
        jnp.arange(row_total, dtype=jnp.int32)[:, None] == rows_of.reshape(-1)[None, :]
    ).astype(jnp.float32)
    added = jnp.stack(
        [
            jnp.dot(
                row_place,
                spread_lines[c],
                precision=lax.Precision.HIGHEST,
                preferred_element_type=jnp.float32,
            )
            for c in range(fields)
        ]
    )
    forced_velocity = predicted + added.reshape(fields, cx, cz, ny)

    forced_wide = halo(forced_velocity, reach, carried=jnp.bfloat16)
    divergence = (
        along_x(forced_wide[0]) + along_y(inner(forced_wide[1])) + along_z(forced_wide[2])
    )
    pressure = inside((neighbours(pressure_wide) - divergence) / 6.0, reach - 1, cz)
    pressure = inside((neighbours(pressure) - inner(divergence)) / 6.0, reach - 2, cz)
    new_velocity = forced_velocity - gradient_of(pressure)
    pressure = inner(pressure)
    return (new_velocity, pressure)


def solution(mesh):
    placed = (
        P(None, "gx", "yz", None),
        P("gx", "yz", None),
        P("gx", "yz", None, None),
        P("gx", "yz", None, None),
        P("gx", "yz", None),
        P("gx", "yz"),
        P("gx", "yz", None),
    )
    return jax.shard_map(
        body,
        mesh=mesh,
        in_specs=placed,
        out_specs=(P(None, "gx", "yz", None), P("gx", "yz", None)),
        check_vma=False,
    )
```

```python
import jax
import jax.numpy as jnp
from jax import lax
from jax.sharding import PartitionSpec as P

BX = 4
BZ = 4
BY = 8
S = 4


step_size = 0.1
viscosity = 1.5


def faces(block, axis, dim, width=1, carried=None):
    count = lax.axis_size(axis)
    forward = [(i, (i + 1) % count) for i in range(count)]
    backward = [(target, source) for source, target in forward]
    kind = carried or block.dtype
    low = lax.ppermute(
        lax.slice_in_dim(block, block.shape[dim] - width, None, axis=dim).astype(kind), axis, forward
    )
    high = lax.ppermute(lax.slice_in_dim(block, 0, width, axis=dim).astype(kind), axis, backward)
    return low.astype(block.dtype), high.astype(block.dtype)


def padded_of(block, x_dim, z_dim, x_faces=None, z_faces=None):
    if x_faces is None:
        x_faces = faces(block, "gx", x_dim)
    if z_faces is None:
        z_faces = faces(block, "yz", z_dim)
    tile_index = lax.axis_index("yz")
    tile_total = lax.axis_size("yz")
    low_z, high_z = z_faces
    low_z = jnp.where(tile_index == 0, jnp.zeros_like(low_z), low_z)
    high_z = jnp.where(tile_index == tile_total - 1, jnp.zeros_like(high_z), high_z)
    middle = jnp.concatenate([low_z, block, high_z], axis=z_dim)
    pad_widths = [(0, 0)] * block.ndim
    pad_widths[z_dim] = (1, 1)
    low_x = jnp.pad(x_faces[0], pad_widths)
    high_x = jnp.pad(x_faces[1], pad_widths)
    return jnp.concatenate([low_x, middle, high_x], axis=x_dim)


def halo(block, width, x_faces=None, carried=None):
    x_total, z_total = block.shape[-3], block.shape[-2]
    low, high = x_faces if x_faces is not None else faces(block, "gx", block.ndim - 3, width, carried)
    grown = jnp.concatenate([low, block, high], axis=-3)
    low, high = faces(grown, "yz", block.ndim - 2, width, carried)
    return inside(jnp.concatenate([low, grown, high], axis=-2), width, z_total)


def inside(field, width, z_total):
    tile_index = lax.axis_index("yz")
    z_count = lax.axis_size("yz")
    position = lax.broadcasted_iota(jnp.int32, field.shape, field.ndim - 2) + tile_index * z_total - width
    valid = jnp.logical_and(position >= 0, position < z_count * z_total)
    return jnp.where(valid, field, jnp.zeros((), field.dtype))


def inner(padded):
    return padded[..., 1:-1, 1:-1, :]


def along_x(padded):
    return 0.5 * (padded[..., 2:, 1:-1, :] - padded[..., :-2, 1:-1, :])


def along_z(padded):
    return 0.5 * (padded[..., 1:-1, 2:, :] - padded[..., 1:-1, :-2, :])


def across_y(field, weights):
    size = field.shape[-1]
    source = lax.broadcasted_iota(jnp.int32, (size, size), 0)
    target = lax.broadcasted_iota(jnp.int32, (size, size), 1)
    above = (source == (target + 1) % size).astype(jnp.float32)
    below = (source == (target + size - 1) % size).astype(jnp.float32)
    matrix = weights[0] * above + weights[1] * below
    return jnp.einsum(
        "...i,ij->...j", field, matrix, precision=lax.Precision.HIGHEST, preferred_element_type=jnp.float32
    )


def along_y(field):
    return across_y(field, (0.5, -0.5))


def neighbours(padded):
    middle = inner(padded)
    total = padded[..., 2:, 1:-1, :] + padded[..., :-2, 1:-1, :]
    total = total + padded[..., 1:-1, 2:, :] + padded[..., 1:-1, :-2, :]
    return total + across_y(middle, (1.0, 1.0))


def gradient_of(padded):
    middle = inner(padded)
    return jnp.stack([along_x(padded), along_y(middle), along_z(padded)])


def predict(flow_padded):
    velocity_padded = flow_padded[:3]
    pressure_padded = flow_padded[3]
    current = inner(velocity_padded)
    laplace = neighbours(velocity_padded) - 6.0 * current
    advect = current[0] * along_x(velocity_padded)
    return current + step_size * (viscosity * laplace - advect) - gradient_of(pressure_padded)


def body(velocity, old_pressure, delta_weight, marker_target, pair_owner, pair_grain, box_anchor):
    fields, cx, cz, ny = velocity.shape
    flow_fields = jnp.concatenate([velocity, old_pressure[None]], 0)
    reach = 3
    low_x, high_x = faces(flow_fields, "gx", 1, reach)
    flow_padded = padded_of(flow_fields, 1, 2, x_faces=(low_x[:, reach - 1 :], high_x[:, :1]))
    predicted = predict(flow_padded)
    pressure_wide = halo(old_pressure, reach, x_faces=(low_x[fields], high_x[fields]))

    anchors = box_anchor[0]
    owners = pair_owner[0, :, 0]
    grains = pair_grain[0]
    delta_weights = delta_weight[0]
    pair_total = anchors.shape[0]
    grain_slots = marker_target.shape[1]
    tiles = lax.axis_size("yz")
    box_rows = BX * BZ
    row_total = cx * cz

    steps = jnp.arange(box_rows, dtype=jnp.int32)
    rows_of = (anchors[:, 0, None] + steps[None, :] // BZ) * cz + anchors[:, 1, None] + steps[None, :] % BZ
    row_select = (
        rows_of.reshape(-1)[:, None] == jnp.arange(row_total, dtype=jnp.int32)[None, :]
    )
    lanes = jnp.arange(ny, dtype=jnp.int32)

    predicted_rows = predicted.astype(jnp.bfloat16).reshape(fields, row_total, ny)
    row_pick = row_select.astype(jnp.bfloat16)
    box_lines = jnp.stack(
        [
            jnp.dot(row_pick, predicted_rows[c], preferred_element_type=jnp.float32)
            for c in range(fields)
        ]
    )
    line_offset = jnp.repeat(anchors[:, 2], box_rows)[:, None]
    window = jnp.stack(
        [jnp.sum(jnp.where(lanes[None, None, :] == line_offset + j, box_lines, 0.0), axis=-1) for j in range(BY)],
        axis=-1,
    )
    kernel_box_values = (
        window.reshape(fields, pair_total, box_rows * BY).transpose(1, 0, 2).astype(jnp.bfloat16)
    )
    partial_force_value = jnp.einsum(
        "pmb,pcb->pcm", delta_weights, kernel_box_values, preferred_element_type=jnp.float32
    )
    row_width = fields * partial_force_value.shape[2]
    flat_partial = partial_force_value.reshape(pair_total, row_width)

    same_owner = owners[:, None] == owners[None, :]
    earlier = jnp.arange(pair_total)[None, :] < jnp.arange(pair_total)[:, None]
    slots = jnp.sum(jnp.logical_and(same_owner, earlier), axis=1).astype(jnp.int32)
    places = owners * S + slots
    dispatch = (jnp.arange(tiles * S, dtype=jnp.int32)[:, None] == places[None, :]).astype(jnp.float32)
    packed = jnp.concatenate(
        [flat_partial, (grains + 1).astype(jnp.float32)[:, None]], axis=1
    )
    send = jnp.dot(
        dispatch, packed, precision=lax.Precision.HIGHEST, preferred_element_type=jnp.float32
    )
    pressure_wide, send = lax.optimization_barrier((pressure_wide, send))
    received = lax.all_to_all(send, "yz", 0, 0, tiled=True)
    received_grain = received[:, row_width]
    received_values = received[:, :row_width]
    slot_numbers = jnp.arange(grain_slots, dtype=jnp.float32) + 1.0
    select = (slot_numbers[:, None] == received_grain[None, :]).astype(jnp.float32)
    summed = jnp.dot(
        select, received_values, precision=lax.Precision.HIGHEST, preferred_element_type=jnp.float32
    )
    targets = marker_target[0].reshape(grain_slots, row_width)
    grain_force = (targets - summed).astype(jnp.bfloat16)
    returned = jnp.einsum(
        "gq,gw->qw", select.astype(jnp.bfloat16), grain_force, preferred_element_type=jnp.float32
    ).astype(jnp.bfloat16)
    back = lax.all_to_all(returned, "yz", 0, 0, tiled=True)
    marker_pair_force = jnp.einsum(
        "qr,qw->rw", dispatch.astype(jnp.bfloat16), back, preferred_element_type=jnp.float32
    ).astype(jnp.bfloat16)

    spread_force = jnp.einsum(
        "pmb,pcm->pcb",
        delta_weights,
        marker_pair_force.reshape(pair_total, fields, -1),
        preferred_element_type=jnp.float32,
    )
    spread_window = spread_force.transpose(1, 0, 2).reshape(fields, pair_total * box_rows, BY)
    spread_lines = sum(
        jnp.where(lanes[None, None, :] == line_offset + j, spread_window[:, :, j, None], 0.0)
        for j in range(BY)
    )
    row_place = (
        jnp.arange(row_total, dtype=jnp.int32)[:, None] == rows_of.reshape(-1)[None, :]
    ).astype(jnp.float32)
    added = jnp.stack(
        [
            jnp.dot(
                row_place,
                spread_lines[c],
                precision=lax.Precision.HIGHEST,
                preferred_element_type=jnp.float32,
            )
            for c in range(fields)
        ]
    )
    forced_velocity = predicted + added.reshape(fields, cx, cz, ny)

    forced_wide = halo(forced_velocity, reach, carried=jnp.bfloat16)
    divergence = (
        along_x(forced_wide[0]) + along_y(inner(forced_wide[1])) + along_z(forced_wide[2])
    )
    pressure = inside((neighbours(pressure_wide) - divergence) / 6.0, reach - 1, cz)
    pressure = inside((neighbours(pressure) - inner(divergence)) / 6.0, reach - 2, cz)
    new_velocity = forced_velocity - gradient_of(pressure)
    pressure = inner(pressure)
    return (new_velocity, pressure)


def solution(mesh):
    placed = (
        P(None, "gx", "yz", None),
        P("gx", "yz", None),
        P("gx", "yz", None, None),
        P("gx", "yz", None, None),
        P("gx", "yz", None),
        P("gx", "yz"),
        P("gx", "yz", None),
    )
    return jax.shard_map(
        body,
        mesh=mesh,
        in_specs=placed,
        out_specs=(P(None, "gx", "yz", None), P("gx", "yz", None)),
        check_vma=False,
    )
```

```python
import jax
import jax.numpy as jnp
from jax import lax
from jax.sharding import PartitionSpec as P

BX = 4
BZ = 4
BY = 8
S = 4


step_size = 0.1
viscosity = 1.5


def faces(block, axis, dim, width=1, carried=None):
    count = lax.axis_size(axis)
    forward = [(i, (i + 1) % count) for i in range(count)]
    backward = [(target, source) for source, target in forward]
    kind = carried or block.dtype
    low = lax.ppermute(
        lax.slice_in_dim(block, block.shape[dim] - width, None, axis=dim).astype(kind), axis, forward
    )
    high = lax.ppermute(lax.slice_in_dim(block, 0, width, axis=dim).astype(kind), axis, backward)
    return low.astype(block.dtype), high.astype(block.dtype)


def padded_of(block, x_dim, z_dim, x_faces=None, z_faces=None):
    if x_faces is None:
        x_faces = faces(block, "gx", x_dim)
    if z_faces is None:
        z_faces = faces(block, "yz", z_dim)
    tile_index = lax.axis_index("yz")
    tile_total = lax.axis_size("yz")
    low_z, high_z = z_faces
    low_z = jnp.where(tile_index == 0, jnp.zeros_like(low_z), low_z)
    high_z = jnp.where(tile_index == tile_total - 1, jnp.zeros_like(high_z), high_z)
    middle = jnp.concatenate([low_z, block, high_z], axis=z_dim)
    pad_widths = [(0, 0)] * block.ndim
    pad_widths[z_dim] = (1, 1)
    low_x = jnp.pad(x_faces[0], pad_widths)
    high_x = jnp.pad(x_faces[1], pad_widths)
    return jnp.concatenate([low_x, middle, high_x], axis=x_dim)


def halo(block, width, x_faces=None, carried=None):
    x_total, z_total = block.shape[-3], block.shape[-2]
    low, high = x_faces if x_faces is not None else faces(block, "gx", block.ndim - 3, width, carried)
    grown = jnp.concatenate([low, block, high], axis=-3)
    low, high = faces(grown, "yz", block.ndim - 2, width, carried)
    return inside(jnp.concatenate([low, grown, high], axis=-2), width, z_total)


def inside(field, width, z_total):
    tile_index = lax.axis_index("yz")
    z_count = lax.axis_size("yz")
    position = lax.broadcasted_iota(jnp.int32, field.shape, field.ndim - 2) + tile_index * z_total - width
    valid = jnp.logical_and(position >= 0, position < z_count * z_total)
    return jnp.where(valid, field, jnp.zeros((), field.dtype))


def inner(padded):
    return padded[..., 1:-1, 1:-1, :]


def along_x(padded):
    return 0.5 * (padded[..., 2:, 1:-1, :] - padded[..., :-2, 1:-1, :])


def along_z(padded):
    return 0.5 * (padded[..., 1:-1, 2:, :] - padded[..., 1:-1, :-2, :])


def across_y(field, weights):
    size = field.shape[-1]
    source = lax.broadcasted_iota(jnp.int32, (size, size), 0)
    target = lax.broadcasted_iota(jnp.int32, (size, size), 1)
    above = (source == (target + 1) % size).astype(jnp.float32)
    below = (source == (target + size - 1) % size).astype(jnp.float32)
    matrix = weights[0] * above + weights[1] * below
    return jnp.einsum(
        "...i,ij->...j", field, matrix, precision=lax.Precision.HIGHEST, preferred_element_type=jnp.float32
    )


def along_y(field):
    return across_y(field, (0.5, -0.5))


def neighbours(padded):
    middle = inner(padded)
    total = padded[..., 2:, 1:-1, :] + padded[..., :-2, 1:-1, :]
    total = total + padded[..., 1:-1, 2:, :] + padded[..., 1:-1, :-2, :]
    return total + across_y(middle, (1.0, 1.0))


def gradient_of(padded):
    middle = inner(padded)
    return jnp.stack([along_x(padded), along_y(middle), along_z(padded)])


def predict(flow_padded):
    velocity_padded = flow_padded[:3]
    pressure_padded = flow_padded[3]
    current = inner(velocity_padded)
    laplace = neighbours(velocity_padded) - 6.0 * current
    advect = current[0] * along_x(velocity_padded)
    return current + step_size * (viscosity * laplace - advect) - gradient_of(pressure_padded)


def body(velocity, old_pressure, delta_weight, marker_target, pair_owner, pair_grain, box_anchor):
    fields, cx, cz, ny = velocity.shape
    flow_fields = jnp.concatenate([velocity, old_pressure[None]], 0)
    reach = 3
    low_x, high_x = faces(flow_fields, "gx", 1, reach)
    flow_padded = padded_of(flow_fields, 1, 2, x_faces=(low_x[:, reach - 1 :], high_x[:, :1]))
    predicted = predict(flow_padded)
    pressure_wide = halo(old_pressure, reach, x_faces=(low_x[fields], high_x[fields]))

    anchors = box_anchor[0]
    owners = pair_owner[0, :, 0]
    grains = pair_grain[0]
    delta_weights = delta_weight[0]
    pair_total = anchors.shape[0]
    grain_slots = marker_target.shape[1]
    tiles = lax.axis_size("yz")
    box_rows = BX * BZ
    row_total = cx * cz

    steps = jnp.arange(box_rows, dtype=jnp.int32)
    rows_of = (anchors[:, 0, None] + steps[None, :] // BZ) * cz + anchors[:, 1, None] + steps[None, :] % BZ
    row_select = (
        rows_of.reshape(-1)[:, None] == jnp.arange(row_total, dtype=jnp.int32)[None, :]
    )
    lanes = jnp.arange(ny, dtype=jnp.int32)

    predicted_rows = predicted.astype(jnp.bfloat16).reshape(fields, row_total, ny)
    row_pick = row_select.astype(jnp.bfloat16)
    box_lines = jnp.stack(
        [
            jnp.dot(row_pick, predicted_rows[c], preferred_element_type=jnp.float32)
            for c in range(fields)
        ]
    )
    line_offset = jnp.repeat(anchors[:, 2], box_rows)[:, None]
    window = jnp.stack(
        [jnp.sum(jnp.where(lanes[None, None, :] == line_offset + j, box_lines, 0.0), axis=-1) for j in range(BY)],
        axis=-1,
    )
    kernel_box_values = (
        window.reshape(fields, pair_total, box_rows * BY).transpose(1, 0, 2).astype(jnp.bfloat16)
    )
    partial_force_value = jnp.einsum(
        "pmb,pcb->pcm", delta_weights, kernel_box_values, preferred_element_type=jnp.float32
    )
    row_width = fields * partial_force_value.shape[2]
    flat_partial = partial_force_value.reshape(pair_total, row_width)

    same_owner = owners[:, None] == owners[None, :]
    earlier = jnp.arange(pair_total)[None, :] < jnp.arange(pair_total)[:, None]
    slots = jnp.sum(jnp.logical_and(same_owner, earlier), axis=1).astype(jnp.int32)
    places = owners * S + slots
    dispatch = (jnp.arange(tiles * S, dtype=jnp.int32)[:, None] == places[None, :]).astype(jnp.float32)
    packed = jnp.concatenate(
        [flat_partial, (grains + 1).astype(jnp.float32)[:, None]], axis=1
    )
    send = jnp.dot(
        dispatch, packed, precision=lax.Precision.HIGHEST, preferred_element_type=jnp.float32
    )
    received = lax.all_to_all(send.reshape(tiles, -1), "yz", 0, 0, tiled=True).reshape(send.shape)
    received_grain = received[:, row_width]
    received_values = received[:, :row_width]
    slot_numbers = jnp.arange(grain_slots, dtype=jnp.float32) + 1.0
    select = (slot_numbers[:, None] == received_grain[None, :]).astype(jnp.float32)
    summed = jnp.dot(
        select, received_values, precision=lax.Precision.HIGHEST, preferred_element_type=jnp.float32
    )
    targets = marker_target[0].reshape(grain_slots, row_width)
    grain_force = (targets - summed).astype(jnp.bfloat16)
    returned = jnp.einsum(
        "gq,gw->qw", select.astype(jnp.bfloat16), grain_force, preferred_element_type=jnp.float32
    ).astype(jnp.bfloat16)
    back = lax.all_to_all(returned, "yz", 0, 0, tiled=True)
    marker_pair_force = jnp.einsum(
        "qr,qw->rw", dispatch.astype(jnp.bfloat16), back, preferred_element_type=jnp.float32
    ).astype(jnp.bfloat16)

    spread_force = jnp.einsum(
        "pmb,pcm->pcb",
        delta_weights,
        marker_pair_force.reshape(pair_total, fields, -1),
        preferred_element_type=jnp.float32,
    )
    spread_window = spread_force.transpose(1, 0, 2).reshape(fields, pair_total * box_rows, BY)
    spread_lines = sum(
        jnp.where(lanes[None, None, :] == line_offset + j, spread_window[:, :, j, None], 0.0)
        for j in range(BY)
    )
    row_place = (
        jnp.arange(row_total, dtype=jnp.int32)[:, None] == rows_of.reshape(-1)[None, :]
    ).astype(jnp.float32)
    added = jnp.stack(
        [
            jnp.dot(
                row_place,
                spread_lines[c],
                precision=lax.Precision.HIGHEST,
                preferred_element_type=jnp.float32,
            )
            for c in range(fields)
        ]
    )
    forced_velocity = predicted + added.reshape(fields, cx, cz, ny)

    forced_wide = halo(forced_velocity, reach, carried=jnp.bfloat16)
    divergence = (
        along_x(forced_wide[0]) + along_y(inner(forced_wide[1])) + along_z(forced_wide[2])
    )
    pressure = inside((neighbours(pressure_wide) - divergence) / 6.0, reach - 1, cz)
    pressure = inside((neighbours(pressure) - inner(divergence)) / 6.0, reach - 2, cz)
    new_velocity = forced_velocity - gradient_of(pressure)
    pressure = inner(pressure)
    return (new_velocity, pressure)


def solution(mesh):
    placed = (
        P(None, "gx", "yz", None),
        P("gx", "yz", None),
        P("gx", "yz", None, None),
        P("gx", "yz", None, None),
        P("gx", "yz", None),
        P("gx", "yz"),
        P("gx", "yz", None),
    )
    return jax.shard_map(
        body,
        mesh=mesh,
        in_specs=placed,
        out_specs=(P(None, "gx", "yz", None), P("gx", "yz", None)),
        check_vma=False,
    )
```

```python
import jax
import jax.numpy as jnp
from jax import lax
from jax.sharding import PartitionSpec as P

BX = 4
BZ = 4
BY = 8
S = 4


step_size = 0.1
viscosity = 1.5


def faces(block, axis, dim, width=1, carried=None):
    count = lax.axis_size(axis)
    forward = [(i, (i + 1) % count) for i in range(count)]
    backward = [(target, source) for source, target in forward]
    kind = carried or block.dtype
    low = lax.ppermute(
        lax.slice_in_dim(block, block.shape[dim] - width, None, axis=dim).astype(kind), axis, forward
    )
    high = lax.ppermute(lax.slice_in_dim(block, 0, width, axis=dim).astype(kind), axis, backward)
    return low.astype(block.dtype), high.astype(block.dtype)


def padded_of(block, x_dim, z_dim, x_faces=None, z_faces=None):
    if x_faces is None:
        x_faces = faces(block, "gx", x_dim)
    if z_faces is None:
        z_faces = faces(block, "yz", z_dim)
    tile_index = lax.axis_index("yz")
    tile_total = lax.axis_size("yz")
    low_z, high_z = z_faces
    low_z = jnp.where(tile_index == 0, jnp.zeros_like(low_z), low_z)
    high_z = jnp.where(tile_index == tile_total - 1, jnp.zeros_like(high_z), high_z)
    middle = jnp.concatenate([low_z, block, high_z], axis=z_dim)
    pad_widths = [(0, 0)] * block.ndim
    pad_widths[z_dim] = (1, 1)
    low_x = jnp.pad(x_faces[0], pad_widths)
    high_x = jnp.pad(x_faces[1], pad_widths)
    return jnp.concatenate([low_x, middle, high_x], axis=x_dim)


def halo(block, width, x_faces=None, carried=None):
    x_total, z_total = block.shape[-3], block.shape[-2]
    low, high = x_faces if x_faces is not None else faces(block, "gx", block.ndim - 3, width, carried)
    grown = jnp.concatenate([low, block, high], axis=-3)
    low, high = faces(grown, "yz", block.ndim - 2, width, carried)
    return inside(jnp.concatenate([low, grown, high], axis=-2), width, z_total)


def inside(field, width, z_total):
    tile_index = lax.axis_index("yz")
    z_count = lax.axis_size("yz")
    position = lax.broadcasted_iota(jnp.int32, field.shape, field.ndim - 2) + tile_index * z_total - width
    valid = jnp.logical_and(position >= 0, position < z_count * z_total)
    return jnp.where(valid, field, jnp.zeros((), field.dtype))


def inner(padded):
    return padded[..., 1:-1, 1:-1, :]


def along_x(padded):
    return 0.5 * (padded[..., 2:, 1:-1, :] - padded[..., :-2, 1:-1, :])


def along_z(padded):
    return 0.5 * (padded[..., 1:-1, 2:, :] - padded[..., 1:-1, :-2, :])


def across_y(field, weights):
    size = field.shape[-1]
    source = lax.broadcasted_iota(jnp.int32, (size, size), 0)
    target = lax.broadcasted_iota(jnp.int32, (size, size), 1)
    above = (source == (target + 1) % size).astype(jnp.float32)
    below = (source == (target + size - 1) % size).astype(jnp.float32)
    matrix = weights[0] * above + weights[1] * below
    return jnp.einsum(
        "...i,ij->...j", field, matrix, precision=lax.Precision.HIGHEST, preferred_element_type=jnp.float32
    )


def along_y(field):
    return across_y(field, (0.5, -0.5))


def neighbours(padded):
    middle = inner(padded)
    total = padded[..., 2:, 1:-1, :] + padded[..., :-2, 1:-1, :]
    total = total + padded[..., 1:-1, 2:, :] + padded[..., 1:-1, :-2, :]
    return total + across_y(middle, (1.0, 1.0))


def gradient_of(padded):
    middle = inner(padded)
    return jnp.stack([along_x(padded), along_y(middle), along_z(padded)])


def predict(flow_padded):
    velocity_padded = flow_padded[:3]
    pressure_padded = flow_padded[3]
    current = inner(velocity_padded)
    laplace = neighbours(velocity_padded) - 6.0 * current
    advect = current[0] * along_x(velocity_padded)
    return current + step_size * (viscosity * laplace - advect) - gradient_of(pressure_padded)


def body(velocity, old_pressure, delta_weight, marker_target, pair_owner, pair_grain, box_anchor):
    fields, cx, cz, ny = velocity.shape
    flow_fields = jnp.concatenate([velocity, old_pressure[None]], 0)
    reach = 3
    low_x, high_x = faces(flow_fields, "gx", 1, reach)
    flow_padded = padded_of(flow_fields, 1, 2, x_faces=(low_x[:, reach - 1 :], high_x[:, :1]))
    predicted = predict(flow_padded)
    pressure_wide = halo(old_pressure, reach, x_faces=(low_x[fields], high_x[fields]))

    anchors = box_anchor[0]
    owners = pair_owner[0, :, 0]
    grains = pair_grain[0]
    delta_weights = delta_weight[0]
    pair_total = anchors.shape[0]
    grain_slots = marker_target.shape[1]
    tiles = lax.axis_size("yz")
    box_rows = BX * BZ
    row_total = cx * cz

    steps = jnp.arange(box_rows, dtype=jnp.int32)
    rows_of = (anchors[:, 0, None] + steps[None, :] // BZ) * cz + anchors[:, 1, None] + steps[None, :] % BZ
    row_select = (
        rows_of.reshape(-1)[:, None] == jnp.arange(row_total, dtype=jnp.int32)[None, :]
    )
    lanes = jnp.arange(ny, dtype=jnp.int32)

    predicted_rows = predicted.astype(jnp.bfloat16).reshape(fields, row_total, ny)
    row_pick = row_select.astype(jnp.bfloat16)
    box_lines = jnp.stack(
        [
            jnp.dot(row_pick, predicted_rows[c], preferred_element_type=jnp.float32)
            for c in range(fields)
        ]
    )
    line_offset = jnp.repeat(anchors[:, 2], box_rows)[:, None]
    window = jnp.stack(
        [jnp.sum(jnp.where(lanes[None, None, :] == line_offset + j, box_lines, 0.0), axis=-1) for j in range(BY)],
        axis=-1,
    )
    kernel_box_values = (
        window.reshape(fields, pair_total, box_rows * BY).transpose(1, 0, 2).astype(jnp.bfloat16)
    )
    partial_force_value = jnp.einsum(
        "pmb,pcb->pcm", delta_weights, kernel_box_values, preferred_element_type=jnp.float32
    )
    row_width = fields * partial_force_value.shape[2]
    flat_partial = partial_force_value.reshape(pair_total, row_width)

    same_owner = owners[:, None] == owners[None, :]
    earlier = jnp.arange(pair_total)[None, :] < jnp.arange(pair_total)[:, None]
    slots = jnp.sum(jnp.logical_and(same_owner, earlier), axis=1).astype(jnp.int32)
    places = owners * S + slots
    dispatch = (jnp.arange(tiles * S, dtype=jnp.int32)[:, None] == places[None, :]).astype(jnp.float32)
    packed = jnp.concatenate(
        [flat_partial, (grains + 1).astype(jnp.float32)[:, None]], axis=1
    )
    send = jnp.dot(
        dispatch, packed, precision=lax.Precision.HIGHEST, preferred_element_type=jnp.float32
    )
    received = lax.all_to_all(send.reshape(tiles, -1), "yz", 0, 0, tiled=True).reshape(send.shape)
    received_grain = received[:, row_width]
    received_values = received[:, :row_width]
    slot_numbers = jnp.arange(grain_slots, dtype=jnp.float32) + 1.0
    select = (slot_numbers[:, None] == received_grain[None, :]).astype(jnp.float32)
    summed = jnp.dot(
        select, received_values, precision=lax.Precision.HIGHEST, preferred_element_type=jnp.float32
    )
    targets = marker_target[0].reshape(grain_slots, row_width)
    grain_force = (targets - summed).astype(jnp.bfloat16)
    returned = jnp.einsum(
        "gq,gw->qw", select.astype(jnp.bfloat16), grain_force, preferred_element_type=jnp.float32
    ).astype(jnp.bfloat16)
    back = lax.all_to_all(returned, "yz", 0, 0, tiled=True)
    marker_pair_force = jnp.einsum(
        "qr,qw->rw", dispatch.astype(jnp.bfloat16), back, preferred_element_type=jnp.float32
    ).astype(jnp.bfloat16)

    spread_force = jnp.einsum(
        "pmb,pcm->pcb",
        delta_weights,
        marker_pair_force.reshape(pair_total, fields, -1),
        preferred_element_type=jnp.float32,
    )
    spread_window = spread_force.transpose(1, 0, 2).reshape(fields, pair_total * box_rows, BY)
    spread_mask = lanes[None, None, :] == line_offset[:, :, None] + jnp.arange(BY, dtype=jnp.int32)[None, :, None]
    spread_lines = jnp.sum(jnp.where(spread_mask[None], spread_window[..., None], 0.0), axis=2)
    row_place = (
        jnp.arange(row_total, dtype=jnp.int32)[:, None] == rows_of.reshape(-1)[None, :]
    ).astype(jnp.float32)
    added = jnp.stack(
        [
            jnp.dot(
                row_place,
                spread_lines[c],
                precision=lax.Precision.HIGHEST,
                preferred_element_type=jnp.float32,
            )
            for c in range(fields)
        ]
    )
    forced_velocity = predicted + added.reshape(fields, cx, cz, ny)

    forced_wide = halo(forced_velocity, reach, carried=jnp.bfloat16)
    divergence = (
        along_x(forced_wide[0]) + along_y(inner(forced_wide[1])) + along_z(forced_wide[2])
    )
    pressure = inside((neighbours(pressure_wide) - divergence) / 6.0, reach - 1, cz)
    pressure = inside((neighbours(pressure) - inner(divergence)) / 6.0, reach - 2, cz)
    new_velocity = forced_velocity - gradient_of(pressure)
    pressure = inner(pressure)
    return (new_velocity, pressure)


def solution(mesh):
    placed = (
        P(None, "gx", "yz", None),
        P("gx", "yz", None),
        P("gx", "yz", None, None),
        P("gx", "yz", None, None),
        P("gx", "yz", None),
        P("gx", "yz"),
        P("gx", "yz", None),
    )
    return jax.shard_map(
        body,
        mesh=mesh,
        in_specs=placed,
        out_specs=(P(None, "gx", "yz", None), P("gx", "yz", None)),
        check_vma=False,
    )
```

```python
import jax
import jax.numpy as jnp
from jax import lax
from jax.sharding import PartitionSpec as P

BX = 4
BZ = 4
BY = 8
S = 4


step_size = 0.1
viscosity = 1.5


def faces(block, axis, dim, width=1, carried=None):
    count = lax.axis_size(axis)
    forward = [(i, (i + 1) % count) for i in range(count)]
    backward = [(target, source) for source, target in forward]
    kind = carried or block.dtype
    low = lax.ppermute(
        lax.slice_in_dim(block, block.shape[dim] - width, None, axis=dim).astype(kind), axis, forward
    )
    high = lax.ppermute(lax.slice_in_dim(block, 0, width, axis=dim).astype(kind), axis, backward)
    return low.astype(block.dtype), high.astype(block.dtype)


def padded_of(block, x_dim, z_dim, x_faces=None, z_faces=None):
    if x_faces is None:
        x_faces = faces(block, "gx", x_dim)
    if z_faces is None:
        z_faces = faces(block, "yz", z_dim)
    tile_index = lax.axis_index("yz")
    tile_total = lax.axis_size("yz")
    low_z, high_z = z_faces
    low_z = jnp.where(tile_index == 0, jnp.zeros_like(low_z), low_z)
    high_z = jnp.where(tile_index == tile_total - 1, jnp.zeros_like(high_z), high_z)
    middle = jnp.concatenate([low_z, block, high_z], axis=z_dim)
    pad_widths = [(0, 0)] * block.ndim
    pad_widths[z_dim] = (1, 1)
    low_x = jnp.pad(x_faces[0], pad_widths)
    high_x = jnp.pad(x_faces[1], pad_widths)
    return jnp.concatenate([low_x, middle, high_x], axis=x_dim)


def halo(block, width, x_faces=None, carried=None):
    x_total, z_total = block.shape[-3], block.shape[-2]
    low, high = x_faces if x_faces is not None else faces(block, "gx", block.ndim - 3, width, carried)
    grown = jnp.concatenate([low, block, high], axis=-3)
    low, high = faces(grown, "yz", block.ndim - 2, width, carried)
    return inside(jnp.concatenate([low, grown, high], axis=-2), width, z_total)


def inside(field, width, z_total):
    tile_index = lax.axis_index("yz")
    z_count = lax.axis_size("yz")
    position = lax.broadcasted_iota(jnp.int32, field.shape, field.ndim - 2) + tile_index * z_total - width
    valid = jnp.logical_and(position >= 0, position < z_count * z_total)
    return jnp.where(valid, field, jnp.zeros((), field.dtype))


def inner(padded):
    return padded[..., 1:-1, 1:-1, :]


def along_x(padded):
    return 0.5 * (padded[..., 2:, 1:-1, :] - padded[..., :-2, 1:-1, :])


def along_z(padded):
    return 0.5 * (padded[..., 1:-1, 2:, :] - padded[..., 1:-1, :-2, :])


def across_y(field, weights):
    size = field.shape[-1]
    source = lax.broadcasted_iota(jnp.int32, (size, size), 0)
    target = lax.broadcasted_iota(jnp.int32, (size, size), 1)
    above = (source == (target + 1) % size).astype(jnp.float32)
    below = (source == (target + size - 1) % size).astype(jnp.float32)
    matrix = weights[0] * above + weights[1] * below
    return jnp.einsum(
        "...i,ij->...j", field, matrix, precision=lax.Precision.HIGH, preferred_element_type=jnp.float32
    )


def along_y(field):
    return across_y(field, (0.5, -0.5))


def neighbours(padded):
    middle = inner(padded)
    total = padded[..., 2:, 1:-1, :] + padded[..., :-2, 1:-1, :]
    total = total + padded[..., 1:-1, 2:, :] + padded[..., 1:-1, :-2, :]
    return total + across_y(middle, (1.0, 1.0))


def gradient_of(padded):
    middle = inner(padded)
    return jnp.stack([along_x(padded), along_y(middle), along_z(padded)])


def predict(flow_padded):
    velocity_padded = flow_padded[:3]
    pressure_padded = flow_padded[3]
    current = inner(velocity_padded)
    laplace = neighbours(velocity_padded) - 6.0 * current
    advect = current[0] * along_x(velocity_padded)
    return current + step_size * (viscosity * laplace - advect) - gradient_of(pressure_padded)


def body(velocity, old_pressure, delta_weight, marker_target, pair_owner, pair_grain, box_anchor):
    fields, cx, cz, ny = velocity.shape
    flow_fields = jnp.concatenate([velocity, old_pressure[None]], 0)
    reach = 3
    low_x, high_x = faces(flow_fields, "gx", 1, reach)
    flow_padded = padded_of(flow_fields, 1, 2, x_faces=(low_x[:, reach - 1 :], high_x[:, :1]))
    predicted = predict(flow_padded)
    pressure_wide = halo(old_pressure, reach, x_faces=(low_x[fields], high_x[fields]))

    anchors = box_anchor[0]
    owners = pair_owner[0, :, 0]
    grains = pair_grain[0]
    delta_weights = delta_weight[0]
    pair_total = anchors.shape[0]
    grain_slots = marker_target.shape[1]
    tiles = lax.axis_size("yz")
    box_rows = BX * BZ
    row_total = cx * cz

    steps = jnp.arange(box_rows, dtype=jnp.int32)
    rows_of = (anchors[:, 0, None] + steps[None, :] // BZ) * cz + anchors[:, 1, None] + steps[None, :] % BZ
    row_select = (
        rows_of.reshape(-1)[:, None] == jnp.arange(row_total, dtype=jnp.int32)[None, :]
    )
    lanes = jnp.arange(ny, dtype=jnp.int32)

    predicted_rows = predicted.astype(jnp.bfloat16).reshape(fields, row_total, ny)
    row_pick = row_select.astype(jnp.bfloat16)
    box_lines = jnp.stack(
        [
            jnp.dot(row_pick, predicted_rows[c], preferred_element_type=jnp.float32)
            for c in range(fields)
        ]
    )
    line_offset = jnp.repeat(anchors[:, 2], box_rows)[:, None]
    window = jnp.stack(
        [jnp.sum(jnp.where(lanes[None, None, :] == line_offset + j, box_lines, 0.0), axis=-1) for j in range(BY)],
        axis=-1,
    )
    kernel_box_values = (
        window.reshape(fields, pair_total, box_rows * BY).transpose(1, 0, 2).astype(jnp.bfloat16)
    )
    partial_force_value = jnp.einsum(
        "pmb,pcb->pcm", delta_weights, kernel_box_values, preferred_element_type=jnp.float32
    )
    row_width = fields * partial_force_value.shape[2]
    flat_partial = partial_force_value.reshape(pair_total, row_width)

    same_owner = owners[:, None] == owners[None, :]
    earlier = jnp.arange(pair_total)[None, :] < jnp.arange(pair_total)[:, None]
    slots = jnp.sum(jnp.logical_and(same_owner, earlier), axis=1).astype(jnp.int32)
    places = owners * S + slots
    dispatch = (jnp.arange(tiles * S, dtype=jnp.int32)[:, None] == places[None, :]).astype(jnp.float32)
    packed = jnp.concatenate(
        [flat_partial, (grains + 1).astype(jnp.float32)[:, None]], axis=1
    )
    send = jnp.dot(
        dispatch, packed, precision=lax.Precision.HIGHEST, preferred_element_type=jnp.float32
    )
    received = lax.all_to_all(send.reshape(tiles, -1), "yz", 0, 0, tiled=True).reshape(send.shape)
    received_grain = received[:, row_width]
    received_values = received[:, :row_width]
    slot_numbers = jnp.arange(grain_slots, dtype=jnp.float32) + 1.0
    select = (slot_numbers[:, None] == received_grain[None, :]).astype(jnp.float32)
    summed = jnp.dot(
        select, received_values, precision=lax.Precision.HIGHEST, preferred_element_type=jnp.float32
    )
    targets = marker_target[0].reshape(grain_slots, row_width)
    grain_force = (targets - summed).astype(jnp.bfloat16)
    returned = jnp.einsum(
        "gq,gw->qw", select.astype(jnp.bfloat16), grain_force, preferred_element_type=jnp.float32
    ).astype(jnp.bfloat16)
    back = lax.all_to_all(returned, "yz", 0, 0, tiled=True)
    marker_pair_force = jnp.einsum(
        "qr,qw->rw", dispatch.astype(jnp.bfloat16), back, preferred_element_type=jnp.float32
    ).astype(jnp.bfloat16)

    spread_force = jnp.einsum(
        "pmb,pcm->pcb",
        delta_weights,
        marker_pair_force.reshape(pair_total, fields, -1),
        preferred_element_type=jnp.float32,
    )
    spread_window = spread_force.transpose(1, 0, 2).reshape(fields, pair_total * box_rows, BY)
    spread_lines = sum(
        jnp.where(lanes[None, None, :] == line_offset + j, spread_window[:, :, j, None], 0.0)
        for j in range(BY)
    )
    row_place = (
        jnp.arange(row_total, dtype=jnp.int32)[:, None] == rows_of.reshape(-1)[None, :]
    ).astype(jnp.float32)
    added = jnp.stack(
        [
            jnp.dot(
                row_place,
                spread_lines[c],
                precision=lax.Precision.HIGHEST,
                preferred_element_type=jnp.float32,
            )
            for c in range(fields)
        ]
    )
    forced_velocity = predicted + added.reshape(fields, cx, cz, ny)

    forced_wide = halo(forced_velocity, reach, carried=jnp.bfloat16)
    divergence = (
        along_x(forced_wide[0]) + along_y(inner(forced_wide[1])) + along_z(forced_wide[2])
    )
    pressure = inside((neighbours(pressure_wide) - divergence) / 6.0, reach - 1, cz)
    pressure = inside((neighbours(pressure) - inner(divergence)) / 6.0, reach - 2, cz)
    new_velocity = forced_velocity - gradient_of(pressure)
    pressure = inner(pressure)
    return (new_velocity, pressure)


def solution(mesh):
    placed = (
        P(None, "gx", "yz", None),
        P("gx", "yz", None),
        P("gx", "yz", None, None),
        P("gx", "yz", None, None),
        P("gx", "yz", None),
        P("gx", "yz"),
        P("gx", "yz", None),
    )
    return jax.shard_map(
        body,
        mesh=mesh,
        in_specs=placed,
        out_specs=(P(None, "gx", "yz", None), P("gx", "yz", None)),
        check_vma=False,
    )
```
